256 devices in a mesh: chan: 64 (over z, y_hi, x), seg: 4 (over y_lo, core).
Axes of the slice: x: 4, y: 4 (y_hi: 2, y_lo: 2; y = y_hi * 2 + y_lo), z: 8, core: 2. Of those that a mesh axis runs over, the one named last changes fastest.
Arguments:
- spectra: bfloat16 [32, 128, 2, 8192], P(None, 'seg', None, 'chan'), may hold values from -6 to 6
- plan: int32 [4, 64], replicated, may hold values from 0 to 63, as said below
- assignment: int32 [8192], P('chan'), may hold values from 0 to 8191, as said below
Outputs:
- cross_spectra: float32 [4, 32, 2, 8192, 128], P(None, 'seg', None, 'chan')
The draws below stay inside these ranges and needn't reach their ends.
Inputs may be any that keep to these rules, and one draw needn't show every extreme that they name: Each row is a pairing of the blocks: plan[r, plan[r, b]] = b and plan[r, b] != b; no two blocks are paired in two different rounds. `assignment`: entries b * 128 to (b + 1) * 128 - 1 are a permutation of that same range of channels.
All inputs are finite; a program needn't handle non-finite values.
Results may differ from the reference program's by a relative error of at most 0.0003.
Values may be sent and summed in bfloat16 or wider, within the bound.
No kernel may reach another device: no remote copies, remote signals or barrier semaphores. Data moves between devices by JAX's collectives and lax.ppermute only.
A program may use at most 128 MiB of HBM per device.

```python
import math
import jax
import jax.numpy as jnp
from jax import lax

CH_BLK = 128
F = 32
ROUNDS = 4
CHANNELS = 8192
WINDOWS = 128
N_CHAN = 64


def draw_plan(key, part):
    group_count = N_CHAN
    odd_count = N_CHAN - 1
    first_key, second_key = jax.random.split(jax.random.fold_in(key, 11))
    round_turns = jax.random.permutation(first_key, odd_count)[:ROUNDS].astype(jnp.int32)
    labels = jax.random.permutation(second_key, group_count).astype(jnp.int32)
    places = jnp.arange(group_count, dtype=jnp.int32)
    mirror = jnp.mod(2 * round_turns[:, None] - places[None, :], odd_count)
    partner_place = jnp.where(places[None, :] == odd_count, round_turns[:, None], jnp.where(mirror == places[None, :], odd_count, mirror))
    sched_table = jnp.zeros((ROUNDS, group_count), jnp.int32).at[:, labels].set(labels[partner_place])
    return sched_table


def draw_assignment(key, part):
    block_keys = jax.random.split(jax.random.fold_in(key, 23), N_CHAN)
    shuffles = jax.vmap(lambda one_key: jax.random.permutation(one_key, CH_BLK))(block_keys)
    offsets = jnp.arange(N_CHAN, dtype=jnp.int32)[:, None] * CH_BLK
    return (shuffles.astype(jnp.int32) + offsets).reshape(N_CHAN * CH_BLK)


def steps_of(key, extent, shards, smallest, high):
    level = 1.0
    for axis_at, shards_of in shards:
        heights = jax.random.uniform(jax.random.fold_in(jax.random.fold_in(key, 6), axis_at), (shards_of,), jnp.float32, smallest / len(shards), high / len(shards))
        level = level * jnp.repeat(jnp.exp(heights), extent[axis_at] // shards_of).reshape((-1,) + (1,) * (len(extent) - 1 - axis_at))
    return level


def scatter_about(rng, shape, scale, limit, cuts=(), kind=jnp.bfloat16):
    drawn = jax.random.normal(rng, shape, jnp.float32) * scale
    if len(cuts) > 0:
        drawn = steps_of(rng, shape, cuts, -0.22, 0.18) * drawn
    return jnp.clip(drawn, min=-limit, max=limit).astype(kind)


def setup_inputs(seed: int = 0) -> dict:
    streams_of = jax.random.split(jax.random.key(seed), 4)
    spectra = scatter_about(streams_of[0], (F, WINDOWS, 2, CHANNELS), 1.0, 6.0, ((1, 4), (3, 64)))
    plan = draw_plan(jax.random.fold_in(streams_of[3], 71), 0)
    assignment = draw_assignment(jax.random.fold_in(streams_of[3], 71), 0)
    return dict(spectra=spectra, plan=plan, assignment=assignment)


def reference(spectra, plan, assignment):
    ordered = jnp.take(spectra, assignment, axis=3)
    scale = 1.0 / math.sqrt(WINDOWS)

    def one_block(pair_index):
        own_block = lax.dynamic_slice_in_dim(ordered, (pair_index[0] * CH_BLK).astype(jnp.int32), CH_BLK, 3).astype(jnp.float32)
        other_block = lax.dynamic_slice_in_dim(ordered, (pair_index[1] * CH_BLK).astype(jnp.int32), CH_BLK, 3).astype(jnp.float32)
        real_part = jnp.einsum('fwc,fwd->fcd', own_block[:, :, 0], other_block[:, :, 0]) + jnp.einsum('fwc,fwd->fcd', own_block[:, :, 1], other_block[:, :, 1])
        imag_part = jnp.einsum('fwc,fwd->fcd', own_block[:, :, 1], other_block[:, :, 0]) - jnp.einsum('fwc,fwd->fcd', own_block[:, :, 0], other_block[:, :, 1])
        return jnp.stack([real_part, imag_part], axis=1) * scale
    rounds_out = []
    for round_index in range(ROUNDS):
        block_ids = jnp.arange(N_CHAN, dtype=jnp.int32)
        blocks = lax.map(one_block, jnp.stack([block_ids, plan[round_index].astype(jnp.int32)], axis=1))
        blocks = jnp.moveaxis(blocks, 0, 2).reshape(F, 2, CHANNELS, CH_BLK)
        rounds_out.append(blocks)
    return jnp.stack(rounds_out)
```

```python
import math

import jax
import jax.numpy as jnp
from jax import lax
from jax.sharding import PartitionSpec as P


def cross_block(own_rows, other_rows, chan_width):
    real_lhs = own_rows
    imag_lhs = jnp.stack([own_rows[:, :, 1], -own_rows[:, :, 0]], axis=2)
    lhs = jnp.stack([real_lhs, imag_lhs], axis=3)
    return jnp.einsum("fwkci,fwkj->fcij", lhs, other_rows, preferred_element_type=jnp.float32)


def on_device(spectra, plan, assignment):
    bin_count, win_local, _, chan_width = spectra.shape
    seg_count = lax.axis_size("seg")
    group_count = lax.axis_size("chan")
    win_count = win_local * seg_count
    scale = 1.0 / math.sqrt(win_count)
    local_slots = assignment - lax.axis_index("chan") * chan_width
    ordered = jnp.take(spectra, local_slots, axis=3)
    own_rows = lax.all_to_all(ordered, "seg", split_axis=0, concat_axis=1, tiled=True)
    my_bins = own_rows.shape[0]
    piece_rows = my_bins * win_count // group_count
    pieces = own_rows.reshape(group_count, piece_rows, 2 * chan_width)
    held = lax.all_to_all(pieces, "chan", split_axis=0, concat_axis=0, tiled=True)
    round_count = plan.shape[0]
    outgoing = jnp.take(held, plan.T, axis=0)
    arrived = lax.all_to_all(outgoing, "chan", split_axis=0, concat_axis=0, tiled=True)
    results = []
    for round_index in range(round_count):
        other_rows = arrived[:, round_index].reshape(my_bins, win_count, 2, chan_width)
        results.append(cross_block(own_rows, other_rows, chan_width) * scale)
    return jnp.stack(results)


def solution(mesh):
    in_specs = (P(None, "seg", None, "chan"), P(), P("chan"))
    out_specs = P(None, "seg", None, "chan", None)
    return jax.shard_map(
        on_device, mesh=mesh, in_specs=in_specs, out_specs=out_specs, check_vma=False
    )
```

```python
import functools
import math

import jax
import jax.numpy as jnp
from jax import lax
from jax.experimental import pallas as pl
from jax.sharding import PartitionSpec as P


def cross_kernel(bins, scale, lhs_ref, rhs_ref, out_ref):
    pieces = rhs_ref.shape[0]
    per_bin = pieces // bins
    chan = out_ref.shape[3]
    for f in range(bins):
        block = rhs_ref[f * per_bin:(f + 1) * per_bin, 0]
        block = block.reshape(per_bin * block.shape[1], block.shape[2])
        acc = jnp.dot(lhs_ref[f, 0], block[:, :chan], preferred_element_type=jnp.float32)
        acc = acc + jnp.dot(lhs_ref[f, 1], block[:, chan:], preferred_element_type=jnp.float32)
        out_ref[0, f] = (acc * scale).reshape(2, chan, chan)


def cross_spectra(lhs, arrived, scale):
    bins, _, two_chan, windows = lhs.shape
    chan = two_chan // 2
    pieces, rounds, rows, _ = arrived.shape
    return pl.pallas_call(
        functools.partial(cross_kernel, bins, scale),
        grid=(rounds,),
        in_specs=[
            pl.BlockSpec((bins, 2, two_chan, windows), lambda r: (0, 0, 0, 0)),
            pl.BlockSpec((pieces, 1, rows, two_chan), lambda r: (0, r, 0, 0)),
        ],
        out_specs=pl.BlockSpec((1, bins, 2, chan, chan), lambda r: (r, 0, 0, 0, 0)),
        out_shape=jax.ShapeDtypeStruct((rounds, bins, 2, chan, chan), jnp.float32),
        cost_estimate=pl.CostEstimate(
            flops=2 * rounds * bins * 2 * two_chan * windows * chan,
            bytes_accessed=lhs.size * 2 + arrived.size * 2 + rounds * bins * 2 * chan * chan * 4,
            transcendentals=0,
        ),
    )(lhs, arrived)


def on_device(spectra, plan, assignment):
    bin_count, win_local, _, chan_width = spectra.shape
    seg_count = lax.axis_size("seg")
    group_count = lax.axis_size("chan")
    seg_index = lax.axis_index("seg")
    win_count = win_local * seg_count
    my_bins = bin_count // seg_count
    scale = 1.0 / math.sqrt(win_count)
    local_slots = assignment - lax.axis_index("chan") * chan_width
    onehot = (local_slots[None, :] == jnp.arange(chan_width, dtype=local_slots.dtype)[:, None])
    ordered = jnp.einsum(
        "fwkm,mc->fwkc", spectra, onehot.astype(spectra.dtype), preferred_element_type=jnp.float32
    ).astype(spectra.dtype)
    per_bin = group_count // my_bins
    win_piece = win_local // per_bin
    rows = ordered.reshape(seg_count, my_bins, per_bin, win_piece, 2 * chan_width)
    send = rows.transpose(1, 2, 0, 3, 4).reshape(group_count * seg_count, win_piece, 2 * chan_width)
    held = lax.all_to_all(send, ("chan", "seg"), split_axis=0, concat_axis=0, tiled=True)
    held = held.reshape(group_count, seg_count * win_piece, 2 * chan_width)
    outgoing = jnp.take(held, plan.T, axis=0)
    arrived = lax.all_to_all(outgoing, "chan", split_axis=0, concat_axis=0, tiled=True)
    ranges = ordered.reshape(seg_count, my_bins, win_local, 2 * chan_width)
    by_shift = [lax.dynamic_index_in_dim(ranges, seg_index, 0, keepdims=False)]
    for shift in range(1, seg_count):
        part = lax.dynamic_index_in_dim(ranges, (seg_index + shift) % seg_count, 0, keepdims=False)
        pairs = [(i, (i + shift) % seg_count) for i in range(seg_count)]
        by_shift.append(lax.ppermute(part, "seg", pairs))
    by_shift = jnp.stack(by_shift)
    order = (seg_index - jnp.arange(seg_count)) % seg_count
    own = jnp.take(by_shift, order, axis=0)
    own = own.reshape(seg_count, my_bins, per_bin, win_piece, 2, chan_width)
    own = own.transpose(1, 4, 5, 2, 0, 3).reshape(my_bins, 2, chan_width, win_count)
    lhs_k0 = jnp.concatenate([own[:, 0], own[:, 1]], axis=1)
    lhs_k1 = jnp.concatenate([own[:, 1], -own[:, 0]], axis=1)
    lhs = jnp.stack([lhs_k0, lhs_k1], axis=1)
    return cross_spectra(lhs, arrived, scale)


def solution(mesh):
    in_specs = (P(None, "seg", None, "chan"), P(), P("chan"))
    out_specs = P(None, "seg", None, "chan", None)
    return jax.shard_map(
        on_device, mesh=mesh, in_specs=in_specs, out_specs=out_specs, check_vma=False
    )
```

```python
import functools
import math

import jax
import jax.numpy as jnp
from jax import lax
from jax.experimental import pallas as pl
from jax.experimental.pallas import tpu as pltpu
from jax.sharding import PartitionSpec as P


def cross_kernel(bins_per_step, scale, lhs_ref, rhs_ref, out_ref):
    step = pl.program_id(0)
    pieces, rounds, rows, two_chan = rhs_ref.shape
    bins = lhs_ref.shape[0]
    per_bin = pieces // bins
    chan = two_chan // 2
    for b in range(bins_per_step):
        f = step * bins_per_step + b
        lhs = lhs_ref[f]
        for r in range(rounds):
            block = rhs_ref[pl.ds(f * per_bin, per_bin), r]
            block = block.reshape(per_bin * rows, two_chan)
            block = jnp.concatenate([block[:, :chan], block[:, chan:]], axis=0)
            acc = jnp.dot(lhs, block, preferred_element_type=jnp.float32)
            out_ref[r, b] = (acc * scale).reshape(2, chan, chan)


def cross_spectra(lhs, arrived, scale):
    bins, two_chan, _ = lhs.shape
    chan = two_chan // 2
    pieces, rounds, rows, _ = arrived.shape
    bins_per_step = 2
    return pl.pallas_call(
        functools.partial(cross_kernel, bins_per_step, scale),
        grid=(bins // bins_per_step,),
        in_specs=[
            pl.BlockSpec(memory_space=pltpu.VMEM),
            pl.BlockSpec(memory_space=pltpu.VMEM),
        ],
        out_specs=pl.BlockSpec((rounds, bins_per_step, 2, chan, chan), lambda g: (0, g, 0, 0, 0)),
        out_shape=jax.ShapeDtypeStruct((rounds, bins, 2, chan, chan), jnp.float32),
        cost_estimate=pl.CostEstimate(
            flops=2 * rounds * bins * two_chan * two_chan * chan,
            bytes_accessed=lhs.size * 2 + arrived.size * 2 + rounds * bins * 2 * chan * chan * 4,
            transcendentals=0,
        ),
    )(lhs, arrived)


def on_device(spectra, plan, assignment):
    bin_count, win_local, _, chan_width = spectra.shape
    seg_count = lax.axis_size("seg")
    group_count = lax.axis_size("chan")
    seg_index = lax.axis_index("seg")
    win_count = win_local * seg_count
    my_bins = bin_count // seg_count
    scale = 1.0 / math.sqrt(win_count)
    local_slots = assignment - lax.axis_index("chan") * chan_width
    onehot = (local_slots[None, :] == jnp.arange(chan_width, dtype=local_slots.dtype)[:, None])
    ordered = jnp.einsum(
        "fwkm,mc->fwkc", spectra, onehot.astype(spectra.dtype), preferred_element_type=jnp.float32
    ).astype(spectra.dtype)
    per_bin = group_count // my_bins
    win_piece = win_local // per_bin
    rows = ordered.reshape(seg_count, my_bins, per_bin, win_piece, 2 * chan_width)
    send = rows.transpose(1, 2, 0, 3, 4).reshape(group_count * seg_count, win_piece, 2 * chan_width)
    round_count = plan.shape[0]
    held = lax.all_to_all(send, ("chan", "seg"), split_axis=0, concat_axis=0, tiled=True)
    held = held.reshape(group_count, seg_count * win_piece, 2 * chan_width)
    pick = plan.T.reshape(-1)[:, None] == jnp.arange(group_count, dtype=plan.dtype)[None, :]
    outgoing = jnp.dot(
        pick.astype(held.dtype), held.reshape(group_count, -1), preferred_element_type=jnp.float32
    ).astype(held.dtype).reshape(group_count, round_count, seg_count * win_piece, 2 * chan_width)
    arrived = lax.all_to_all(outgoing, "chan", split_axis=0, concat_axis=0, tiled=True)
    ranges = ordered.reshape(seg_count, my_bins, win_local, 2 * chan_width)
    by_shift = [lax.dynamic_index_in_dim(ranges, seg_index, 0, keepdims=False)]
    for shift in range(1, seg_count):
        part = lax.dynamic_index_in_dim(ranges, (seg_index + shift) % seg_count, 0, keepdims=False)
        pairs = [(i, (i + shift) % seg_count) for i in range(seg_count)]
        by_shift.append(lax.ppermute(part, "seg", pairs))
    by_shift = jnp.stack(by_shift)
    order = (seg_index - jnp.arange(seg_count)) % seg_count
    own = jnp.take(by_shift, order, axis=0)
    own = own.reshape(seg_count, my_bins, per_bin, win_piece, 2, chan_width)
    own = own.transpose(1, 5, 4, 2, 0, 3).reshape(my_bins, chan_width, 2, win_count)
    imag_rows = jnp.stack([own[:, :, 1], -own[:, :, 0]], axis=2)
    lhs = jnp.stack([own, imag_rows], axis=1).reshape(my_bins, 2 * chan_width, 2 * win_count)
    return cross_spectra(lhs, arrived, scale)


def solution(mesh):
    in_specs = (P(None, "seg", None, "chan"), P(), P("chan"))
    out_specs = P(None, "seg", None, "chan", None)
    return jax.shard_map(
        on_device, mesh=mesh, in_specs=in_specs, out_specs=out_specs, check_vma=False
    )
```

```python
import functools
import math

import jax
import jax.numpy as jnp
from jax import lax
from jax.experimental import pallas as pl
from jax.sharding import PartitionSpec as P


def cross_kernel(scale, lhs_ref, rhs_ref, out_ref):
    per_bin, rounds, rows, two_chan = rhs_ref.shape
    chan = two_chan // 2
    columns = []
    for r in range(rounds):
        block = rhs_ref[:, r].reshape(per_bin * rows, two_chan)
        columns.append(jnp.concatenate([block[:, :chan], block[:, chan:]], axis=0))
    rhs = jnp.concatenate(columns, axis=1)
    acc = jnp.dot(lhs_ref[0], rhs, preferred_element_type=jnp.float32) * scale
    for r in range(rounds):
        out_ref[r, 0] = acc[:, r * chan:(r + 1) * chan].reshape(2, chan, chan)


def cross_spectra(lhs, arrived, scale):
    bins, two_chan, two_win = lhs.shape
    chan = two_chan // 2
    pieces, rounds, rows, _ = arrived.shape
    per_bin = pieces // bins
    return pl.pallas_call(
        functools.partial(cross_kernel, scale),
        grid=(bins,),
        in_specs=[
            pl.BlockSpec((1, two_chan, two_win), lambda f: (f, 0, 0)),
            pl.BlockSpec((per_bin, rounds, rows, two_chan), lambda f: (f, 0, 0, 0)),
        ],
        out_specs=pl.BlockSpec((rounds, 1, 2, chan, chan), lambda f: (0, f, 0, 0, 0)),
        out_shape=jax.ShapeDtypeStruct((rounds, bins, 2, chan, chan), jnp.float32),
        cost_estimate=pl.CostEstimate(
            flops=2 * rounds * bins * two_chan * two_win * chan,
            bytes_accessed=lhs.size * 2 + arrived.size * 2 + rounds * bins * 2 * chan * chan * 4,
            transcendentals=0,
        ),
    )(lhs, arrived)


def on_device(spectra, plan, assignment):
    bin_count, win_local, _, chan_width = spectra.shape
    seg_count = lax.axis_size("seg")
    group_count = lax.axis_size("chan")
    seg_index = lax.axis_index("seg")
    win_count = win_local * seg_count
    my_bins = bin_count // seg_count
    scale = 1.0 / math.sqrt(win_count)
    local_slots = assignment - lax.axis_index("chan") * chan_width
    onehot = (local_slots[None, :] == jnp.arange(chan_width, dtype=local_slots.dtype)[:, None])
    ordered = jnp.einsum(
        "fwkm,mc->fwkc", spectra, onehot.astype(spectra.dtype), preferred_element_type=jnp.float32
    ).astype(spectra.dtype)
    per_bin = group_count // my_bins
    win_piece = win_local // per_bin
    rows = ordered.reshape(seg_count, my_bins, per_bin, win_piece, 2 * chan_width)
    send = rows.transpose(1, 2, 0, 3, 4).reshape(group_count * seg_count, win_piece, 2 * chan_width)
    held = lax.all_to_all(send, ("chan", "seg"), split_axis=0, concat_axis=0, tiled=True)
    held = held.reshape(group_count, seg_count * win_piece, 2 * chan_width)
    outgoing = held.at[plan.T].get(mode="promise_in_bounds")
    arrived = lax.all_to_all(outgoing, "chan", split_axis=0, concat_axis=0, tiled=True)
    ranges = ordered.reshape(seg_count, my_bins, win_local, 2 * chan_width)
    by_shift = [lax.dynamic_index_in_dim(ranges, seg_index, 0, keepdims=False)]
    for shift in range(1, seg_count):
        part = lax.dynamic_index_in_dim(ranges, (seg_index + shift) % seg_count, 0, keepdims=False)
        pairs = [(i, (i + shift) % seg_count) for i in range(seg_count)]
        by_shift.append(lax.ppermute(part, "seg", pairs))
    by_shift = jnp.stack(by_shift)
    order = (seg_index - jnp.arange(seg_count)) % seg_count
    own = jnp.take(by_shift, order, axis=0)
    own = own.reshape(seg_count, my_bins, per_bin, win_piece, 2, chan_width)
    own = own.transpose(1, 5, 4, 2, 0, 3).reshape(my_bins, chan_width, 2, win_count)
    imag_rows = jnp.stack([own[:, :, 1], -own[:, :, 0]], axis=2)
    lhs = jnp.stack([own, imag_rows], axis=1).reshape(my_bins, 2 * chan_width, 2 * win_count)
    return cross_spectra(lhs, arrived, scale)


def solution(mesh):
    in_specs = (P(None, "seg", None, "chan"), P(), P("chan"))
    out_specs = P(None, "seg", None, "chan", None)
    return jax.shard_map(
        on_device, mesh=mesh, in_specs=in_specs, out_specs=out_specs, check_vma=False
    )
```

```python
import functools
import math

import jax
import jax.numpy as jnp
from jax import lax
from jax.experimental import pallas as pl
from jax.experimental.pallas import tpu as pltpu
from jax.sharding import PartitionSpec as P


def cross_kernel(bins_per_step, scale, lhs_ref, rhs_ref, out_ref):
    step = pl.program_id(0)
    pieces, rounds, rows, two_chan = rhs_ref.shape
    bins = lhs_ref.shape[0]
    per_bin = pieces // bins
    chan = two_chan // 2
    for b in range(bins_per_step):
        f = step * bins_per_step + b
        lhs = lhs_ref[f]
        for r in range(rounds):
            block = rhs_ref[pl.ds(f * per_bin, per_bin), r]
            block = block.reshape(per_bin * rows, two_chan)
            block = jnp.concatenate([block[:, :chan], block[:, chan:]], axis=0)
            acc = jnp.dot(lhs, block, preferred_element_type=jnp.float32)
            out_ref[r, b] = (acc * scale).reshape(2, chan, chan)


def cross_spectra(lhs, arrived, scale):
    bins, two_chan, _ = lhs.shape
    chan = two_chan // 2
    pieces, rounds, rows, _ = arrived.shape
    bins_per_step = 2
    return pl.pallas_call(
        functools.partial(cross_kernel, bins_per_step, scale),
        grid=(bins // bins_per_step,),
        in_specs=[
            pl.BlockSpec(memory_space=pltpu.VMEM),
            pl.BlockSpec(memory_space=pltpu.VMEM),
        ],
        out_specs=pl.BlockSpec((rounds, bins_per_step, 2, chan, chan), lambda g: (0, g, 0, 0, 0)),
        out_shape=jax.ShapeDtypeStruct((rounds, bins, 2, chan, chan), jnp.float32),
        cost_estimate=pl.CostEstimate(
            flops=2 * rounds * bins * two_chan * two_chan * chan,
            bytes_accessed=lhs.size * 2 + arrived.size * 2 + rounds * bins * 2 * chan * chan * 4,
            transcendentals=0,
        ),
    )(lhs, arrived)


def on_device(spectra, plan, assignment):
    bin_count, win_local, _, chan_width = spectra.shape
    seg_count = lax.axis_size("seg")
    group_count = lax.axis_size("chan")
    seg_index = lax.axis_index("seg")
    win_count = win_local * seg_count
    my_bins = bin_count // seg_count
    scale = 1.0 / math.sqrt(win_count)
    local_slots = assignment - lax.axis_index("chan") * chan_width
    onehot = (local_slots[None, :] == jnp.arange(chan_width, dtype=local_slots.dtype)[:, None])
    ordered = jnp.einsum(
        "fwkm,mc->fwkc", spectra, onehot.astype(spectra.dtype), preferred_element_type=jnp.float32
    ).astype(spectra.dtype)
    per_bin = group_count // my_bins
    win_piece = win_local // per_bin
    rows = ordered.reshape(seg_count, my_bins, per_bin, win_piece, 2 * chan_width)
    send = rows.transpose(1, 2, 0, 3, 4).reshape(group_count * seg_count, win_piece, 2 * chan_width)
    held = lax.all_to_all(send, ("chan", "seg"), split_axis=0, concat_axis=0, tiled=True)
    held = held.reshape(group_count, seg_count * win_piece, 2 * chan_width)
    outgoing = held.at[plan.T].get(mode="promise_in_bounds")
    arrived = lax.all_to_all(outgoing, "chan", split_axis=0, concat_axis=0, tiled=True)
    ranges = ordered.reshape(seg_count, my_bins, win_local, 2 * chan_width)
    by_shift = [lax.dynamic_index_in_dim(ranges, seg_index, 0, keepdims=False)]
    for shift in range(1, seg_count):
        part = lax.dynamic_index_in_dim(ranges, (seg_index + shift) % seg_count, 0, keepdims=False)
        pairs = [(i, (i + shift) % seg_count) for i in range(seg_count)]
        by_shift.append(lax.ppermute(part, "seg", pairs))
    by_shift = jnp.stack(by_shift)
    order = (seg_index - jnp.arange(seg_count)) % seg_count
    own = jnp.take(by_shift, order, axis=0)
    own = own.reshape(seg_count, my_bins, per_bin, win_piece, 2, chan_width)
    own = own.transpose(1, 5, 4, 2, 0, 3).reshape(my_bins, chan_width, 2, win_count)
    imag_rows = jnp.stack([own[:, :, 1], -own[:, :, 0]], axis=2)
    lhs = jnp.stack([own, imag_rows], axis=1).reshape(my_bins, 2 * chan_width, 2 * win_count)
    return cross_spectra(lhs, arrived, scale)


def solution(mesh):
    in_specs = (P(None, "seg", None, "chan"), P(), P("chan"))
    out_specs = P(None, "seg", None, "chan", None)
    return jax.shard_map(
        on_device, mesh=mesh, in_specs=in_specs, out_specs=out_specs, check_vma=False
    )
```

```python
import functools
import math

import jax
import jax.numpy as jnp
from jax import lax
from jax.experimental import pallas as pl
from jax.sharding import PartitionSpec as P


def cross_kernel(scale, lhs_ref, rhs_ref, out_ref):
    step_bins = lhs_ref.shape[0]
    pieces, rounds, rows, two_chan = rhs_ref.shape
    per_bin = pieces // step_bins
    chan = two_chan // 2
    for b in range(step_bins):
        lhs = lhs_ref[b]
        for r in range(rounds):
            block = rhs_ref[b * per_bin:(b + 1) * per_bin, r].reshape(per_bin * rows, two_chan)
            block = jnp.concatenate([block[:, :chan], block[:, chan:]], axis=0)
            acc = jnp.dot(lhs, block, preferred_element_type=jnp.float32)
            out_ref[r, b] = (acc * scale).reshape(2, chan, chan)


def cross_spectra(lhs, arrived, scale):
    bins, two_chan, two_win = lhs.shape
    chan = two_chan // 2
    pieces, rounds, rows, _ = arrived.shape
    per_bin = pieces // bins
    step_bins = 4
    return pl.pallas_call(
        functools.partial(cross_kernel, scale),
        grid=(bins // step_bins,),
        in_specs=[
            pl.BlockSpec((step_bins, two_chan, two_win), lambda g: (g, 0, 0)),
            pl.BlockSpec((step_bins * per_bin, rounds, rows, two_chan), lambda g: (g, 0, 0, 0)),
        ],
        out_specs=pl.BlockSpec((rounds, step_bins, 2, chan, chan), lambda g: (0, g, 0, 0, 0)),
        out_shape=jax.ShapeDtypeStruct((rounds, bins, 2, chan, chan), jnp.float32),
        cost_estimate=pl.CostEstimate(
            flops=2 * rounds * bins * two_chan * two_win * chan,
            bytes_accessed=lhs.size * 2 + arrived.size * 2 + rounds * bins * 2 * chan * chan * 4,
            transcendentals=0,
        ),
    )(lhs, arrived)


def on_device(spectra, plan, assignment):
    bin_count, win_local, _, chan_width = spectra.shape
    seg_count = lax.axis_size("seg")
    group_count = lax.axis_size("chan")
    seg_index = lax.axis_index("seg")
    win_count = win_local * seg_count
    my_bins = bin_count // seg_count
    scale = 1.0 / math.sqrt(win_count)
    local_slots = assignment - lax.axis_index("chan") * chan_width
    onehot = (local_slots[None, :] == jnp.arange(chan_width, dtype=local_slots.dtype)[:, None])
    ordered = jnp.einsum(
        "fwkm,mc->fwkc", spectra, onehot.astype(spectra.dtype), preferred_element_type=jnp.float32
    ).astype(spectra.dtype)
    per_bin = group_count // my_bins
    win_piece = win_local // per_bin
    rows = ordered.reshape(seg_count, my_bins, per_bin, win_piece, 2 * chan_width)
    send = rows.transpose(1, 2, 0, 3, 4).reshape(group_count * seg_count, win_piece, 2 * chan_width)
    held = lax.all_to_all(send, ("chan", "seg"), split_axis=0, concat_axis=0, tiled=True)
    held = held.reshape(group_count, seg_count * win_piece, 2 * chan_width)
    outgoing = held.at[plan.T].get(mode="promise_in_bounds")
    arrived = lax.all_to_all(outgoing, "chan", split_axis=0, concat_axis=0, tiled=True)
    ranges = ordered.reshape(seg_count, my_bins, win_local, 2 * chan_width)
    by_shift = [lax.dynamic_index_in_dim(ranges, seg_index, 0, keepdims=False)]
    for shift in range(1, seg_count):
        part = lax.dynamic_index_in_dim(ranges, (seg_index + shift) % seg_count, 0, keepdims=False)
        pairs = [(i, (i + shift) % seg_count) for i in range(seg_count)]
        by_shift.append(lax.ppermute(part, "seg", pairs))
    by_shift = jnp.stack(by_shift)
    order = (seg_index - jnp.arange(seg_count)) % seg_count
    own = jnp.take(by_shift, order, axis=0)
    own = own.reshape(seg_count, my_bins, per_bin, win_piece, 2, chan_width)
    own = own.transpose(1, 5, 4, 2, 0, 3).reshape(my_bins, chan_width, 2, win_count)
    imag_rows = jnp.stack([own[:, :, 1], -own[:, :, 0]], axis=2)
    lhs = jnp.stack([own, imag_rows], axis=1).reshape(my_bins, 2 * chan_width, 2 * win_count)
    return cross_spectra(lhs, arrived, scale)


def solution(mesh):
    in_specs = (P(None, "seg", None, "chan"), P(), P("chan"))
    out_specs = P(None, "seg", None, "chan", None)
    return jax.shard_map(
        on_device, mesh=mesh, in_specs=in_specs, out_specs=out_specs, check_vma=False
    )
```

```python
import functools
import math

import jax
import jax.numpy as jnp
from jax import lax
from jax.experimental import pallas as pl
from jax.sharding import PartitionSpec as P


def cross_kernel(scale, lhs_ref, rhs_ref, out_ref):
    step_bins = lhs_ref.shape[0]
    pieces, rounds, rows, two_chan = rhs_ref.shape
    per_bin = pieces // step_bins
    chan = two_chan // 2
    for b in range(step_bins):
        lhs = lhs_ref[b]
        for r in range(rounds):
            block = rhs_ref[b * per_bin:(b + 1) * per_bin, r].reshape(per_bin * rows, two_chan)
            block = jnp.concatenate([block[:, :chan], block[:, chan:]], axis=0)
            acc = jnp.dot(lhs, block, preferred_element_type=jnp.float32)
            out_ref[r, b] = (acc * scale).reshape(2, chan, chan)


def cross_spectra(lhs, arrived, scale):
    bins, two_chan, two_win = lhs.shape
    chan = two_chan // 2
    pieces, rounds, rows, _ = arrived.shape
    per_bin = pieces // bins
    step_bins = 4
    return pl.pallas_call(
        functools.partial(cross_kernel, scale),
        grid=(bins // step_bins,),
        in_specs=[
            pl.BlockSpec((step_bins, two_chan, two_win), lambda g: (g, 0, 0)),
            pl.BlockSpec((step_bins * per_bin, rounds, rows, two_chan), lambda g: (g, 0, 0, 0)),
        ],
        out_specs=pl.BlockSpec((rounds, step_bins, 2, chan, chan), lambda g: (0, g, 0, 0, 0)),
        out_shape=jax.ShapeDtypeStruct((rounds, bins, 2, chan, chan), jnp.float32),
        cost_estimate=pl.CostEstimate(
            flops=2 * rounds * bins * two_chan * two_win * chan,
            bytes_accessed=lhs.size * 2 + arrived.size * 2 + rounds * bins * 2 * chan * chan * 4,
            transcendentals=0,
        ),
    )(lhs, arrived)


def on_device(spectra, plan, assignment):
    bin_count, win_local, _, chan_width = spectra.shape
    seg_count = lax.axis_size("seg")
    group_count = lax.axis_size("chan")
    seg_index = lax.axis_index("seg")
    win_count = win_local * seg_count
    my_bins = bin_count // seg_count
    scale = 1.0 / math.sqrt(win_count)
    local_slots = assignment - lax.axis_index("chan") * chan_width
    onehot = (local_slots[None, :] == jnp.arange(chan_width, dtype=local_slots.dtype)[:, None])
    ordered = jnp.einsum(
        "fwkm,mc->fwkc", spectra, onehot.astype(spectra.dtype), preferred_element_type=jnp.float32
    ).astype(spectra.dtype)
    per_bin = group_count // my_bins
    win_piece = win_local // per_bin
    send = ordered.reshape(seg_count * group_count, win_piece, 2 * chan_width)
    held = lax.all_to_all(send, ("seg", "chan"), split_axis=0, concat_axis=0, tiled=True)
    sources = (jnp.arange(seg_count, dtype=plan.dtype) * group_count)[None, None, :] + plan.T[:, :, None]
    outgoing = held.at[sources].get(mode="promise_in_bounds")
    outgoing = outgoing.reshape(group_count, plan.shape[0], seg_count * win_piece, 2 * chan_width)
    arrived = lax.all_to_all(outgoing, "chan", split_axis=0, concat_axis=0, tiled=True)
    ranges = ordered.reshape(seg_count, my_bins, win_local, 2 * chan_width)
    by_shift = [lax.dynamic_index_in_dim(ranges, seg_index, 0, keepdims=False)]
    for shift in range(1, seg_count):
        part = lax.dynamic_index_in_dim(ranges, (seg_index + shift) % seg_count, 0, keepdims=False)
        pairs = [(i, (i + shift) % seg_count) for i in range(seg_count)]
        by_shift.append(lax.ppermute(part, "seg", pairs))
    by_shift = jnp.stack(by_shift)
    order = (seg_index - jnp.arange(seg_count)) % seg_count
    own = jnp.take(by_shift, order, axis=0)
    own = own.reshape(seg_count, my_bins, per_bin, win_piece, 2, chan_width)
    own = own.transpose(1, 5, 4, 2, 0, 3).reshape(my_bins, chan_width, 2, win_count)
    imag_rows = jnp.stack([own[:, :, 1], -own[:, :, 0]], axis=2)
    lhs = jnp.stack([own, imag_rows], axis=1).reshape(my_bins, 2 * chan_width, 2 * win_count)
    return cross_spectra(lhs, arrived, scale)


def solution(mesh):
    in_specs = (P(None, "seg", None, "chan"), P(), P("chan"))
    out_specs = P(None, "seg", None, "chan", None)
    return jax.shard_map(
        on_device, mesh=mesh, in_specs=in_specs, out_specs=out_specs, check_vma=False
    )
```

```python
import functools
import math

import jax
import jax.numpy as jnp
from jax import lax
from jax.experimental import pallas as pl
from jax.experimental.pallas import tpu as pltpu
from jax.sharding import PartitionSpec as P


def cross_kernel(scale, lhs_ref, rhs_ref, out_ref):
    step_bins = lhs_ref.shape[0]
    pieces, rounds, rows, two_chan = rhs_ref.shape
    per_bin = pieces // (step_bins * pl.num_programs(0))
    chan = two_chan // 2
    first = pl.program_id(0) * step_bins
    for b in range(step_bins):
        lhs = lhs_ref[b]
        for r in range(rounds):
            block = rhs_ref[pl.ds((first + b) * per_bin, per_bin), r]
            block = block.reshape(per_bin * rows, two_chan)
            block = jnp.concatenate([block[:, :chan], block[:, chan:]], axis=0)
            acc = jnp.dot(lhs, block, preferred_element_type=jnp.float32)
            out_ref[r, b] = (acc * scale).reshape(2, chan, chan)


def cross_spectra(lhs, arrived, scale):
    bins, two_chan, two_win = lhs.shape
    chan = two_chan // 2
    pieces, rounds, rows, _ = arrived.shape
    per_bin = pieces // bins
    step_bins = 4
    return pl.pallas_call(
        functools.partial(cross_kernel, scale),
        grid=(bins // step_bins,),
        in_specs=[
            pl.BlockSpec((step_bins, two_chan, two_win), lambda g: (g, 0, 0)),
            pl.BlockSpec(memory_space=pltpu.VMEM),
        ],
        out_specs=pl.BlockSpec((rounds, step_bins, 2, chan, chan), lambda g: (0, g, 0, 0, 0)),
        out_shape=jax.ShapeDtypeStruct((rounds, bins, 2, chan, chan), jnp.float32),
        cost_estimate=pl.CostEstimate(
            flops=2 * rounds * bins * two_chan * two_win * chan,
            bytes_accessed=lhs.size * 2 + arrived.size * 2 + rounds * bins * 2 * chan * chan * 4,
            transcendentals=0,
        ),
    )(lhs, pltpu.with_memory_space_constraint(arrived, pltpu.VMEM))


def on_device(spectra, plan, assignment):
    bin_count, win_local, _, chan_width = spectra.shape
    seg_count = lax.axis_size("seg")
    group_count = lax.axis_size("chan")
    seg_index = lax.axis_index("seg")
    win_count = win_local * seg_count
    my_bins = bin_count // seg_count
    scale = 1.0 / math.sqrt(win_count)
    local_slots = assignment - lax.axis_index("chan") * chan_width
    onehot = (local_slots[None, :] == jnp.arange(chan_width, dtype=local_slots.dtype)[:, None])
    ordered = jnp.einsum(
        "fwkm,mc->fwkc", spectra, onehot.astype(spectra.dtype), preferred_element_type=jnp.float32
    ).astype(spectra.dtype)
    per_bin = group_count // my_bins
    win_piece = win_local // per_bin
    rows = ordered.reshape(seg_count, my_bins, per_bin, win_piece, 2 * chan_width)
    send = rows.transpose(1, 2, 0, 3, 4).reshape(group_count * seg_count, win_piece, 2 * chan_width)
    held = lax.all_to_all(send, ("chan", "seg"), split_axis=0, concat_axis=0, tiled=True)
    held = held.reshape(group_count, seg_count * win_piece, 2 * chan_width)
    outgoing = held.at[plan.T].get(mode="promise_in_bounds")
    arrived = lax.all_to_all(outgoing, "chan", split_axis=0, concat_axis=0, tiled=True)
    ranges = ordered.reshape(seg_count, my_bins, win_local, 2 * chan_width)
    by_shift = [lax.dynamic_index_in_dim(ranges, seg_index, 0, keepdims=False)]
    for shift in range(1, seg_count):
        part = lax.dynamic_index_in_dim(ranges, (seg_index + shift) % seg_count, 0, keepdims=False)
        pairs = [(i, (i + shift) % seg_count) for i in range(seg_count)]
        by_shift.append(lax.ppermute(part, "seg", pairs))
    by_shift = jnp.stack(by_shift)
    order = (seg_index - jnp.arange(seg_count)) % seg_count
    own = jnp.take(by_shift, order, axis=0)
    own = own.reshape(seg_count, my_bins, per_bin, win_piece, 2, chan_width)
    own = own.transpose(1, 5, 4, 2, 0, 3).reshape(my_bins, chan_width, 2, win_count)
    imag_rows = jnp.stack([own[:, :, 1], -own[:, :, 0]], axis=2)
    lhs = jnp.stack([own, imag_rows], axis=1).reshape(my_bins, 2 * chan_width, 2 * win_count)
    return cross_spectra(lhs, arrived, scale)


def solution(mesh):
    in_specs = (P(None, "seg", None, "chan"), P(), P("chan"))
    out_specs = P(None, "seg", None, "chan", None)
    return jax.shard_map(
        on_device, mesh=mesh, in_specs=in_specs, out_specs=out_specs, check_vma=False
    )
```

```python
import functools
import math

import jax
import jax.numpy as jnp
from jax import lax
from jax.experimental import pallas as pl
from jax.experimental.pallas import tpu as pltpu
from jax.sharding import PartitionSpec as P


def cross_kernel(scale, lhs_hbm, rhs_ref, out_hbm, lhs_buf, out_buf, lhs_sems, out_sems):
    bins = lhs_buf.shape[0]
    pieces, rounds, rows, two_chan = rhs_ref.shape
    per_bin = pieces // bins
    chan = two_chan // 2
    lhs_copies = [
        pltpu.make_async_copy(lhs_hbm.at[f], lhs_buf.at[f], lhs_sems.at[f]) for f in range(bins)
    ]
    for copy in lhs_copies:
        copy.start()
    out_copies = []
    for f in range(bins):
        lhs_copies[f].wait()
        lhs = lhs_buf[f]
        for r in range(rounds):
            block = rhs_ref[f * per_bin:(f + 1) * per_bin, r].reshape(per_bin * rows, two_chan)
            block = jnp.concatenate([block[:, :chan], block[:, chan:]], axis=0)
            acc = jnp.dot(lhs, block, preferred_element_type=jnp.float32)
            out_buf[r, f] = (acc * scale).reshape(2, chan, chan)
            copy = pltpu.make_async_copy(out_buf.at[r, f], out_hbm.at[r, f], out_sems.at[r, f])
            copy.start()
            out_copies.append(copy)
    for copy in out_copies:
        copy.wait()


def cross_spectra(lhs, arrived, scale):
    bins, two_chan, two_win = lhs.shape
    chan = two_chan // 2
    pieces, rounds, rows, _ = arrived.shape
    return pl.pallas_call(
        functools.partial(cross_kernel, scale),
        in_specs=[
            pl.BlockSpec(memory_space=pl.ANY),
            pl.BlockSpec(memory_space=pltpu.VMEM),
        ],
        out_specs=pl.BlockSpec(memory_space=pl.ANY),
        out_shape=jax.ShapeDtypeStruct((rounds, bins, 2, chan, chan), jnp.float32),
        scratch_shapes=[
            pltpu.VMEM(lhs.shape, lhs.dtype),
            pltpu.VMEM((rounds, bins, 2, chan, chan), jnp.float32),
            pltpu.SemaphoreType.DMA((bins,)),
            pltpu.SemaphoreType.DMA((rounds, bins)),
        ],
        cost_estimate=pl.CostEstimate(
            flops=2 * rounds * bins * two_chan * two_win * chan,
            bytes_accessed=lhs.size * 2 + arrived.size * 2 + rounds * bins * 2 * chan * chan * 4,
            transcendentals=0,
        ),
    )(lhs, pltpu.with_memory_space_constraint(arrived, pltpu.VMEM))


def on_device(spectra, plan, assignment):
    bin_count, win_local, _, chan_width = spectra.shape
    seg_count = lax.axis_size("seg")
    group_count = lax.axis_size("chan")
    seg_index = lax.axis_index("seg")
    win_count = win_local * seg_count
    my_bins = bin_count // seg_count
    scale = 1.0 / math.sqrt(win_count)
    local_slots = assignment - lax.axis_index("chan") * chan_width
    onehot = (local_slots[None, :] == jnp.arange(chan_width, dtype=local_slots.dtype)[:, None])
    ordered = jnp.einsum(
        "fwkm,mc->fwkc", spectra, onehot.astype(spectra.dtype), preferred_element_type=jnp.float32
    ).astype(spectra.dtype)
    per_bin = group_count // my_bins
    win_piece = win_local // per_bin
    rows = ordered.reshape(seg_count, my_bins, per_bin, win_piece, 2 * chan_width)
    send = rows.transpose(1, 2, 0, 3, 4).reshape(group_count * seg_count, win_piece, 2 * chan_width)
    held = lax.all_to_all(send, ("chan", "seg"), split_axis=0, concat_axis=0, tiled=True)
    held = held.reshape(group_count, seg_count * win_piece, 2 * chan_width)
    outgoing = held.at[plan.T].get(mode="promise_in_bounds")
    arrived = lax.all_to_all(outgoing, "chan", split_axis=0, concat_axis=0, tiled=True)
    ranges = ordered.reshape(seg_count, my_bins, win_local, 2 * chan_width)
    by_shift = [lax.dynamic_index_in_dim(ranges, seg_index, 0, keepdims=False)]
    for shift in range(1, seg_count):
        part = lax.dynamic_index_in_dim(ranges, (seg_index + shift) % seg_count, 0, keepdims=False)
        pairs = [(i, (i + shift) % seg_count) for i in range(seg_count)]
        by_shift.append(lax.ppermute(part, "seg", pairs))
    by_shift = jnp.stack(by_shift)
    order = (seg_index - jnp.arange(seg_count)) % seg_count
    own = jnp.take(by_shift, order, axis=0)
    own = own.reshape(seg_count, my_bins, per_bin, win_piece, 2, chan_width)
    own = own.transpose(1, 5, 4, 2, 0, 3).reshape(my_bins, chan_width, 2, win_count)
    imag_rows = jnp.stack([own[:, :, 1], -own[:, :, 0]], axis=2)
    lhs = jnp.stack([own, imag_rows], axis=1).reshape(my_bins, 2 * chan_width, 2 * win_count)
    return cross_spectra(lhs, arrived, scale)


def solution(mesh):
    in_specs = (P(None, "seg", None, "chan"), P(), P("chan"))
    out_specs = P(None, "seg", None, "chan", None)
    return jax.shard_map(
        on_device, mesh=mesh, in_specs=in_specs, out_specs=out_specs, check_vma=False
    )
```

```python
import functools
import math

import jax
import jax.numpy as jnp
from jax import lax
from jax.experimental import pallas as pl
from jax.experimental.pallas import tpu as pltpu
from jax.sharding import PartitionSpec as P


def cross_kernel(scale, lhs_ref, rhs_ref, out_ref):
    step_bins = lhs_ref.shape[0]
    pieces, rounds, rows, two_chan = rhs_ref.shape
    per_bin = pieces // (step_bins * pl.num_programs(0))
    chan = two_chan // 2
    first = pl.program_id(0) * step_bins
    for b in range(step_bins):
        lhs = lhs_ref[b]
        for r in range(rounds):
            block = rhs_ref[pl.ds((first + b) * per_bin, per_bin), r]
            block = block.reshape(per_bin * rows, two_chan)
            block = jnp.concatenate([block[:, :chan], block[:, chan:]], axis=0)
            acc = jnp.dot(lhs, block, preferred_element_type=jnp.float32)
            out_ref[r, b] = (acc * scale).reshape(2, chan, chan)


def cross_spectra(lhs, arrived, scale):
    bins, two_chan, two_win = lhs.shape
    chan = two_chan // 2
    pieces, rounds, rows, _ = arrived.shape
    per_bin = pieces // bins
    step_bins = 2
    return pl.pallas_call(
        functools.partial(cross_kernel, scale),
        grid=(bins // step_bins,),
        in_specs=[
            pl.BlockSpec((step_bins, two_chan, two_win), lambda g: (g, 0, 0)),
            pl.BlockSpec(memory_space=pltpu.VMEM),
        ],
        out_specs=pl.BlockSpec((rounds, step_bins, 2, chan, chan), lambda g: (0, g, 0, 0, 0)),
        out_shape=jax.ShapeDtypeStruct((rounds, bins, 2, chan, chan), jnp.float32),
        cost_estimate=pl.CostEstimate(
            flops=2 * rounds * bins * two_chan * two_win * chan,
            bytes_accessed=lhs.size * 2 + arrived.size * 2 + rounds * bins * 2 * chan * chan * 4,
            transcendentals=0,
        ),
    )(lhs, pltpu.with_memory_space_constraint(arrived, pltpu.VMEM))


def on_device(spectra, plan, assignment):
    bin_count, win_local, _, chan_width = spectra.shape
    seg_count = lax.axis_size("seg")
    group_count = lax.axis_size("chan")
    seg_index = lax.axis_index("seg")
    win_count = win_local * seg_count
    my_bins = bin_count // seg_count
    scale = 1.0 / math.sqrt(win_count)
    local_slots = assignment - lax.axis_index("chan") * chan_width
    onehot = (local_slots[None, :] == jnp.arange(chan_width, dtype=local_slots.dtype)[:, None])
    ordered = jnp.einsum(
        "fwkm,mc->fwkc", spectra, onehot.astype(spectra.dtype), preferred_element_type=jnp.float32
    ).astype(spectra.dtype)
    per_bin = group_count // my_bins
    win_piece = win_local // per_bin
    rows = ordered.reshape(seg_count, my_bins, per_bin, win_piece, 2 * chan_width)
    send = rows.transpose(1, 2, 0, 3, 4).reshape(group_count * seg_count, win_piece, 2 * chan_width)
    held = lax.all_to_all(send, ("chan", "seg"), split_axis=0, concat_axis=0, tiled=True)
    held = held.reshape(group_count, seg_count * win_piece, 2 * chan_width)
    outgoing = held.at[plan.T].get(mode="promise_in_bounds")
    arrived = lax.all_to_all(outgoing, "chan", split_axis=0, concat_axis=0, tiled=True)
    ranges = ordered.reshape(seg_count, my_bins, win_local, 2 * chan_width)
    by_shift = [lax.dynamic_index_in_dim(ranges, seg_index, 0, keepdims=False)]
    for shift in range(1, seg_count):
        part = lax.dynamic_index_in_dim(ranges, (seg_index + shift) % seg_count, 0, keepdims=False)
        pairs = [(i, (i + shift) % seg_count) for i in range(seg_count)]
        by_shift.append(lax.ppermute(part, "seg", pairs))
    by_shift = jnp.stack(by_shift)
    order = (seg_index - jnp.arange(seg_count)) % seg_count
    own = jnp.take(by_shift, order, axis=0)
    own = own.reshape(seg_count, my_bins, per_bin, win_piece, 2, chan_width)
    own = own.transpose(1, 5, 4, 2, 0, 3).reshape(my_bins, chan_width, 2, win_count)
    imag_rows = jnp.stack([own[:, :, 1], -own[:, :, 0]], axis=2)
    lhs = jnp.stack([own, imag_rows], axis=1).reshape(my_bins, 2 * chan_width, 2 * win_count)
    return cross_spectra(lhs, arrived, scale)


def solution(mesh):
    in_specs = (P(None, "seg", None, "chan"), P(), P("chan"))
    out_specs = P(None, "seg", None, "chan", None)
    return jax.shard_map(
        on_device, mesh=mesh, in_specs=in_specs, out_specs=out_specs, check_vma=False
    )
```

```python
import functools
import math

import jax
import jax.numpy as jnp
from jax import lax
from jax.experimental import pallas as pl
from jax.experimental.pallas import tpu as pltpu
from jax.sharding import PartitionSpec as P


def cross_kernel(scale, lhs_ref, rhs_ref, out_ref):
    step_bins = lhs_ref.shape[0]
    pieces, rounds, rows, two_chan = rhs_ref.shape
    per_bin = pieces // (step_bins * pl.num_programs(0))
    chan = two_chan // 2
    first = pl.program_id(0) * step_bins
    for b in range(step_bins):
        lhs = lhs_ref[b]
        for r in range(rounds):
            block = rhs_ref[pl.ds((first + b) * per_bin, per_bin), r]
            block = block.reshape(per_bin * rows, two_chan)
            block = jnp.concatenate([block[:, :chan], block[:, chan:]], axis=0)
            acc = jnp.dot(lhs, block, preferred_element_type=jnp.float32)
            out_ref[r, b] = (acc * scale).reshape(2, chan, chan)


def cross_spectra(lhs, arrived, scale):
    bins, two_chan, two_win = lhs.shape
    chan = two_chan // 2
    pieces, rounds, rows, _ = arrived.shape
    per_bin = pieces // bins
    step_bins = 4
    return pl.pallas_call(
        functools.partial(cross_kernel, scale),
        grid=(bins // step_bins,),
        in_specs=[
            pl.BlockSpec((step_bins, two_chan, two_win), lambda g: (g, 0, 0)),
            pl.BlockSpec(memory_space=pltpu.VMEM),
        ],
        out_specs=pl.BlockSpec((rounds, step_bins, 2, chan, chan), lambda g: (0, g, 0, 0, 0)),
        out_shape=jax.ShapeDtypeStruct((rounds, bins, 2, chan, chan), jnp.float32),
        cost_estimate=pl.CostEstimate(
            flops=2 * rounds * bins * two_chan * two_win * chan,
            bytes_accessed=lhs.size * 2 + arrived.size * 2 + rounds * bins * 2 * chan * chan * 4,
            transcendentals=0,
        ),
    )(lhs, pltpu.with_memory_space_constraint(arrived, pltpu.VMEM))


def on_device(spectra, plan, assignment):
    bin_count, win_local, _, chan_width = spectra.shape
    seg_count = lax.axis_size("seg")
    group_count = lax.axis_size("chan")
    seg_index = lax.axis_index("seg")
    win_count = win_local * seg_count
    my_bins = bin_count // seg_count
    scale = 1.0 / math.sqrt(win_count)
    local_slots = assignment - lax.axis_index("chan") * chan_width
    onehot = (local_slots[None, :] == jnp.arange(chan_width, dtype=local_slots.dtype)[:, None])
    per_bin = group_count // my_bins
    win_piece = win_local // per_bin
    pieces = spectra.reshape(seg_count, my_bins, per_bin, win_piece, 2, chan_width).transpose(1, 2, 0, 3, 4, 5)
    send = jnp.einsum(
        "fqsrkm,mc->fqsrkc", pieces, onehot.astype(spectra.dtype), preferred_element_type=jnp.float32
    ).astype(spectra.dtype).reshape(group_count * seg_count, win_piece, 2 * chan_width)
    held = lax.all_to_all(send, ("chan", "seg"), split_axis=0, concat_axis=0, tiled=True)
    held = held.reshape(group_count, seg_count * win_piece, 2 * chan_width)
    outgoing = held.at[plan.T].get(mode="promise_in_bounds")
    arrived = lax.all_to_all(outgoing, "chan", split_axis=0, concat_axis=0, tiled=True)
    ordered = jnp.einsum(
        "fwkm,mc->fwkc", spectra, onehot.astype(spectra.dtype), preferred_element_type=jnp.float32
    ).astype(spectra.dtype)
    ranges = ordered.reshape(seg_count, my_bins, win_local, 2 * chan_width)
    by_shift = [lax.dynamic_index_in_dim(ranges, seg_index, 0, keepdims=False)]
    for shift in range(1, seg_count):
        part = lax.dynamic_index_in_dim(ranges, (seg_index + shift) % seg_count, 0, keepdims=False)
        pairs = [(i, (i + shift) % seg_count) for i in range(seg_count)]
        by_shift.append(lax.ppermute(part, "seg", pairs))
    by_shift = jnp.stack(by_shift)
    order = (seg_index - jnp.arange(seg_count)) % seg_count
    own = jnp.take(by_shift, order, axis=0)
    own = own.reshape(seg_count, my_bins, per_bin, win_piece, 2, chan_width)
    own = own.transpose(1, 5, 4, 2, 0, 3).reshape(my_bins, chan_width, 2, win_count)
    imag_rows = jnp.stack([own[:, :, 1], -own[:, :, 0]], axis=2)
    lhs = jnp.stack([own, imag_rows], axis=1).reshape(my_bins, 2 * chan_width, 2 * win_count)
    return cross_spectra(lhs, arrived, scale)


def solution(mesh):
    in_specs = (P(None, "seg", None, "chan"), P(), P("chan"))
    out_specs = P(None, "seg", None, "chan", None)
    return jax.shard_map(
        on_device, mesh=mesh, in_specs=in_specs, out_specs=out_specs, check_vma=False
    )
```

```python
import functools
import math

import jax
import jax.numpy as jnp
from jax import lax
from jax.experimental import pallas as pl
from jax.experimental.pallas import tpu as pltpu
from jax.sharding import PartitionSpec as P


def cross_kernel(scale, lhs_ref, rhs_ref, out_ref):
    step_bins = lhs_ref.shape[0]
    pieces, rounds, rows, chan = rhs_ref.shape
    per_bin = pieces // (step_bins * pl.num_programs(0))
    first = pl.program_id(0) * step_bins
    for b in range(step_bins):
        lhs = lhs_ref[b]
        for r in range(rounds):
            block = rhs_ref[pl.ds((first + b) * per_bin, per_bin), r]
            block = block.reshape(per_bin * rows, chan)
            acc = jnp.dot(lhs, block, preferred_element_type=jnp.float32)
            out_ref[r, b] = (acc * scale).reshape(2, chan, chan)


def cross_spectra(lhs, arrived, scale):
    bins, two_chan, two_win = lhs.shape
    chan = two_chan // 2
    pieces, rounds, rows, _ = arrived.shape
    per_bin = pieces // bins
    step_bins = 4
    return pl.pallas_call(
        functools.partial(cross_kernel, scale),
        grid=(bins // step_bins,),
        in_specs=[
            pl.BlockSpec((step_bins, two_chan, two_win), lambda g: (g, 0, 0)),
            pl.BlockSpec(memory_space=pltpu.VMEM),
        ],
        out_specs=pl.BlockSpec((rounds, step_bins, 2, chan, chan), lambda g: (0, g, 0, 0, 0)),
        out_shape=jax.ShapeDtypeStruct((rounds, bins, 2, chan, chan), jnp.float32),
        cost_estimate=pl.CostEstimate(
            flops=2 * rounds * bins * two_chan * two_win * chan,
            bytes_accessed=lhs.size * 2 + arrived.size * 2 + rounds * bins * 2 * chan * chan * 4,
            transcendentals=0,
        ),
    )(lhs, pltpu.with_memory_space_constraint(arrived, pltpu.VMEM))


def on_device(spectra, plan, assignment):
    bin_count, win_local, _, chan_width = spectra.shape
    seg_count = lax.axis_size("seg")
    group_count = lax.axis_size("chan")
    seg_index = lax.axis_index("seg")
    win_count = win_local * seg_count
    my_bins = bin_count // seg_count
    scale = 1.0 / math.sqrt(win_count)
    local_slots = assignment - lax.axis_index("chan") * chan_width
    onehot = (local_slots[None, :] == jnp.arange(chan_width, dtype=local_slots.dtype)[:, None])
    ordered = jnp.einsum(
        "fwkm,mc->fwkc", spectra, onehot.astype(spectra.dtype), preferred_element_type=jnp.float32
    ).astype(spectra.dtype)
    per_bin = group_count // my_bins
    win_piece = win_local // per_bin
    rows = ordered.reshape(seg_count, my_bins, per_bin, win_piece, 2 * chan_width)
    send = rows.transpose(1, 2, 0, 3, 4).reshape(group_count * seg_count, win_piece * 2, chan_width)
    held = lax.all_to_all(send, ("chan", "seg"), split_axis=0, concat_axis=0, tiled=True)
    held = held.reshape(group_count, seg_count * win_piece * 2, chan_width)
    outgoing = held.at[plan.T].get(mode="promise_in_bounds")
    arrived = lax.all_to_all(outgoing, "chan", split_axis=0, concat_axis=0, tiled=True)
    ranges = ordered.reshape(seg_count, my_bins, win_local, 2 * chan_width)
    by_shift = [lax.dynamic_index_in_dim(ranges, seg_index, 0, keepdims=False)]
    for shift in range(1, seg_count):
        part = lax.dynamic_index_in_dim(ranges, (seg_index + shift) % seg_count, 0, keepdims=False)
        pairs = [(i, (i + shift) % seg_count) for i in range(seg_count)]
        by_shift.append(lax.ppermute(part, "seg", pairs))
    by_shift = jnp.stack(by_shift)
    order = (seg_index - jnp.arange(seg_count)) % seg_count
    own = jnp.take(by_shift, order, axis=0)
    own = own.reshape(seg_count, my_bins, per_bin, win_piece, 2, chan_width)
    imag_rows = jnp.stack([own[:, :, :, :, 1], -own[:, :, :, :, 0]], axis=4)
    lhs = jnp.stack([own, imag_rows], axis=0).transpose(2, 0, 6, 3, 1, 4, 5)
    lhs = lhs.reshape(my_bins, 2 * chan_width, 2 * win_count)
    return cross_spectra(lhs, arrived, scale)


def solution(mesh):
    in_specs = (P(None, "seg", None, "chan"), P(), P("chan"))
    out_specs = P(None, "seg", None, "chan", None)
    return jax.shard_map(
        on_device, mesh=mesh, in_specs=in_specs, out_specs=out_specs, check_vma=False
    )
```

```python
import functools
import math

import jax
import jax.numpy as jnp
from jax import lax
from jax.experimental import pallas as pl
from jax.experimental.pallas import tpu as pltpu
from jax.sharding import PartitionSpec as P


def cross_kernel(scale, lhs_ref, rhs_ref, out_ref):
    step_bins = lhs_ref.shape[0]
    pieces, rounds, rows, two_chan = rhs_ref.shape
    per_bin = pieces // (step_bins * pl.num_programs(0))
    chan = two_chan // 2
    first = pl.program_id(0) * step_bins
    for b in range(step_bins):
        lhs = lhs_ref[b]
        for r in range(rounds):
            block = rhs_ref[pl.ds((first + b) * per_bin, per_bin), r]
            block = block.reshape(per_bin * rows, two_chan)
            block = jnp.concatenate([block[:, :chan], block[:, chan:]], axis=0)
            acc = jnp.dot(lhs, block, preferred_element_type=jnp.float32)
            out_ref[r, b] = (acc * scale).reshape(2, chan, chan)


def cross_spectra(lhs, arrived, scale):
    bins, two_chan, two_win = lhs.shape
    chan = two_chan // 2
    pieces, rounds, rows, _ = arrived.shape
    per_bin = pieces // bins
    step_bins = 4
    return pl.pallas_call(
        functools.partial(cross_kernel, scale),
        grid=(bins // step_bins,),
        in_specs=[
            pl.BlockSpec((step_bins, two_chan, two_win), lambda g: (g, 0, 0)),
            pl.BlockSpec(memory_space=pltpu.VMEM),
        ],
        out_specs=pl.BlockSpec((rounds, step_bins, 2, chan, chan), lambda g: (0, g, 0, 0, 0)),
        out_shape=jax.ShapeDtypeStruct((rounds, bins, 2, chan, chan), jnp.float32),
        cost_estimate=pl.CostEstimate(
            flops=2 * rounds * bins * two_chan * two_win * chan,
            bytes_accessed=lhs.size * 2 + arrived.size * 2 + rounds * bins * 2 * chan * chan * 4,
            transcendentals=0,
        ),
    )(lhs, pltpu.with_memory_space_constraint(arrived, pltpu.VMEM))


def pick_kernel(plan_ref, held_ref, out_ref):
    step_dests, rounds = out_ref.shape[0], out_ref.shape[1]
    first = pl.program_id(0) * step_dests
    for d in range(step_dests):
        for r in range(rounds):
            out_ref[d, r] = held_ref[plan_ref[r, first + d]]


def pick_partners(plan, held):
    rounds, dests = plan.shape
    _, rows, width = held.shape
    step_dests = 16
    return pl.pallas_call(
        pick_kernel,
        grid_spec=pltpu.PrefetchScalarGridSpec(
            num_scalar_prefetch=1,
            grid=(dests // step_dests,),
            in_specs=[pl.BlockSpec(memory_space=pltpu.VMEM)],
            out_specs=pl.BlockSpec((step_dests, rounds, rows, width), lambda g, plan_ref: (g, 0, 0, 0)),
        ),
        out_shape=jax.ShapeDtypeStruct((dests, rounds, rows, width), held.dtype),
        cost_estimate=pl.CostEstimate(
            flops=0, bytes_accessed=held.size * 2 + dests * rounds * rows * width * 4, transcendentals=0
        ),
    )(plan, pltpu.with_memory_space_constraint(held, pltpu.VMEM))


def on_device(spectra, plan, assignment):
    bin_count, win_local, _, chan_width = spectra.shape
    seg_count = lax.axis_size("seg")
    group_count = lax.axis_size("chan")
    seg_index = lax.axis_index("seg")
    win_count = win_local * seg_count
    my_bins = bin_count // seg_count
    scale = 1.0 / math.sqrt(win_count)
    local_slots = assignment - lax.axis_index("chan") * chan_width
    onehot = (local_slots[None, :] == jnp.arange(chan_width, dtype=local_slots.dtype)[:, None])
    ordered = jnp.einsum(
        "fwkm,mc->fwkc", spectra, onehot.astype(spectra.dtype), preferred_element_type=jnp.float32
    ).astype(spectra.dtype)
    per_bin = group_count // my_bins
    win_piece = win_local // per_bin
    rows = ordered.reshape(seg_count, my_bins, per_bin, win_piece, 2 * chan_width)
    send = rows.transpose(1, 2, 0, 3, 4).reshape(group_count * seg_count, win_piece, 2 * chan_width)
    held = lax.all_to_all(send, ("chan", "seg"), split_axis=0, concat_axis=0, tiled=True)
    held = held.reshape(group_count, seg_count * win_piece, 2 * chan_width)
    outgoing = pick_partners(plan, held)
    arrived = lax.all_to_all(outgoing, "chan", split_axis=0, concat_axis=0, tiled=True)
    ranges = ordered.reshape(seg_count, my_bins, win_local, 2 * chan_width)
    by_shift = [lax.dynamic_index_in_dim(ranges, seg_index, 0, keepdims=False)]
    for shift in range(1, seg_count):
        part = lax.dynamic_index_in_dim(ranges, (seg_index + shift) % seg_count, 0, keepdims=False)
        pairs = [(i, (i + shift) % seg_count) for i in range(seg_count)]
        by_shift.append(lax.ppermute(part, "seg", pairs))
    by_shift = jnp.stack(by_shift)
    order = (seg_index - jnp.arange(seg_count)) % seg_count
    own = jnp.take(by_shift, order, axis=0)
    own = own.reshape(seg_count, my_bins, per_bin, win_piece, 2, chan_width)
    own = own.transpose(1, 5, 4, 2, 0, 3).reshape(my_bins, chan_width, 2, win_count)
    imag_rows = jnp.stack([own[:, :, 1], -own[:, :, 0]], axis=2)
    lhs = jnp.stack([own, imag_rows], axis=1).reshape(my_bins, 2 * chan_width, 2 * win_count)
    return cross_spectra(lhs, arrived, scale)


def solution(mesh):
    in_specs = (P(None, "seg", None, "chan"), P(), P("chan"))
    out_specs = P(None, "seg", None, "chan", None)
    return jax.shard_map(
        on_device, mesh=mesh, in_specs=in_specs, out_specs=out_specs, check_vma=False
    )
```

```python
import functools
import math

import jax
import jax.numpy as jnp
from jax import lax
from jax.experimental import pallas as pl
from jax.experimental.pallas import tpu as pltpu
from jax.sharding import PartitionSpec as P


def cross_kernel(scale, lhs_ref, rhs_ref, out_ref):
    step_bins = lhs_ref.shape[0]
    pieces, rounds, rows, two_chan = rhs_ref.shape
    per_bin = pieces // (step_bins * pl.num_programs(0))
    chan = two_chan // 2
    first = pl.program_id(0) * step_bins
    for b in range(step_bins):
        lhs = lhs_ref[b]
        for r in range(rounds):
            block = rhs_ref[pl.ds((first + b) * per_bin, per_bin), r]
            block = block.reshape(per_bin * rows, two_chan)
            block = jnp.concatenate([block[:, :chan], block[:, chan:]], axis=0)
            acc = jnp.dot(lhs, block, preferred_element_type=jnp.float32)
            out_ref[r, b] = (acc * scale).reshape(2, chan, chan)


def cross_spectra(lhs, arrived, scale):
    bins, two_chan, two_win = lhs.shape
    chan = two_chan // 2
    pieces, rounds, rows, _ = arrived.shape
    per_bin = pieces // bins
    step_bins = 4
    return pl.pallas_call(
        functools.partial(cross_kernel, scale),
        grid=(bins // step_bins,),
        in_specs=[
            pl.BlockSpec((step_bins, two_chan, two_win), lambda g: (g, 0, 0)),
            pl.BlockSpec(memory_space=pltpu.VMEM),
        ],
        out_specs=pl.BlockSpec((rounds, step_bins, 2, chan, chan), lambda g: (0, g, 0, 0, 0)),
        out_shape=jax.ShapeDtypeStruct((rounds, bins, 2, chan, chan), jnp.float32),
        cost_estimate=pl.CostEstimate(
            flops=2 * rounds * bins * two_chan * two_win * chan,
            bytes_accessed=lhs.size * 2 + arrived.size * 2 + rounds * bins * 2 * chan * chan * 4,
            transcendentals=0,
        ),
    )(lhs, pltpu.with_memory_space_constraint(arrived, pltpu.VMEM))


def pick_kernel(plan_ref, held_ref, out_ref):
    dests, rounds = out_ref.shape[0], out_ref.shape[1]
    for d in range(dests):
        for r in range(rounds):
            out_ref[d, r] = held_ref[plan_ref[r, d]]


def pick_partners(plan, held):
    rounds, dests = plan.shape
    _, rows, width = held.shape
    return pl.pallas_call(
        pick_kernel,
        in_specs=[pl.BlockSpec(memory_space=pltpu.SMEM), pl.BlockSpec(memory_space=pltpu.VMEM)],
        out_specs=pl.BlockSpec(memory_space=pltpu.VMEM),
        out_shape=jax.ShapeDtypeStruct((dests, rounds, rows, width), held.dtype),
        cost_estimate=pl.CostEstimate(
            flops=0, bytes_accessed=held.size * 2 + dests * rounds * rows * width * 4, transcendentals=0
        ),
    )(plan, pltpu.with_memory_space_constraint(held, pltpu.VMEM))


def on_device(spectra, plan, assignment):
    bin_count, win_local, _, chan_width = spectra.shape
    seg_count = lax.axis_size("seg")
    group_count = lax.axis_size("chan")
    seg_index = lax.axis_index("seg")
    win_count = win_local * seg_count
    my_bins = bin_count // seg_count
    scale = 1.0 / math.sqrt(win_count)
    local_slots = assignment - lax.axis_index("chan") * chan_width
    onehot = (local_slots[None, :] == jnp.arange(chan_width, dtype=local_slots.dtype)[:, None])
    ordered = jnp.einsum(
        "fwkm,mc->fwkc", spectra, onehot.astype(spectra.dtype), preferred_element_type=jnp.float32
    ).astype(spectra.dtype)
    per_bin = group_count // my_bins
    win_piece = win_local // per_bin
    rows = ordered.reshape(seg_count, my_bins, per_bin, win_piece, 2 * chan_width)
    send = rows.transpose(1, 2, 0, 3, 4).reshape(group_count * seg_count, win_piece, 2 * chan_width)
    held = lax.all_to_all(send, ("chan", "seg"), split_axis=0, concat_axis=0, tiled=True)
    held = held.reshape(group_count, seg_count * win_piece, 2 * chan_width)
    outgoing = pick_partners(plan, held)
    arrived = lax.all_to_all(outgoing, "chan", split_axis=0, concat_axis=0, tiled=True)
    ranges = ordered.reshape(seg_count, my_bins, win_local, 2 * chan_width)
    by_shift = [lax.dynamic_index_in_dim(ranges, seg_index, 0, keepdims=False)]
    for shift in range(1, seg_count):
        part = lax.dynamic_index_in_dim(ranges, (seg_index + shift) % seg_count, 0, keepdims=False)
        pairs = [(i, (i + shift) % seg_count) for i in range(seg_count)]
        by_shift.append(lax.ppermute(part, "seg", pairs))
    by_shift = jnp.stack(by_shift)
    order = (seg_index - jnp.arange(seg_count)) % seg_count
    own = jnp.take(by_shift, order, axis=0)
    own = own.reshape(seg_count, my_bins, per_bin, win_piece, 2, chan_width)
    own = own.transpose(1, 5, 4, 2, 0, 3).reshape(my_bins, chan_width, 2, win_count)
    imag_rows = jnp.stack([own[:, :, 1], -own[:, :, 0]], axis=2)
    lhs = jnp.stack([own, imag_rows], axis=1).reshape(my_bins, 2 * chan_width, 2 * win_count)
    return cross_spectra(lhs, arrived, scale)


def solution(mesh):
    in_specs = (P(None, "seg", None, "chan"), P(), P("chan"))
    out_specs = P(None, "seg", None, "chan", None)
    return jax.shard_map(
        on_device, mesh=mesh, in_specs=in_specs, out_specs=out_specs, check_vma=False
    )
```

```python
import functools
import math

import jax
import jax.numpy as jnp
from jax import lax
from jax.experimental import pallas as pl
from jax.experimental.pallas import tpu as pltpu
from jax.sharding import PartitionSpec as P


def cross_kernel(scale, lhs_ref, rhs_ref, out_ref):
    step_bins = lhs_ref.shape[0]
    pieces, rounds, rows, two_chan = rhs_ref.shape
    per_bin = pieces // (step_bins * pl.num_programs(0))
    chan = two_chan // 2
    first = pl.program_id(0) * step_bins
    for b in range(step_bins):
        lhs = lhs_ref[b]
        for r in range(rounds):
            block = rhs_ref[pl.ds((first + b) * per_bin, per_bin), r]
            block = block.reshape(per_bin * rows, two_chan)
            block = jnp.concatenate([block[:, :chan], block[:, chan:]], axis=0)
            acc = jnp.dot(lhs, block, preferred_element_type=jnp.float32)
            out_ref[r, b] = (acc * scale).reshape(2, chan, chan)


def cross_spectra(lhs, arrived, scale):
    bins, two_chan, two_win = lhs.shape
    chan = two_chan // 2
    pieces, rounds, rows, _ = arrived.shape
    per_bin = pieces // bins
    step_bins = 4
    return pl.pallas_call(
        functools.partial(cross_kernel, scale),
        grid=(bins // step_bins,),
        in_specs=[
            pl.BlockSpec((step_bins, two_chan, two_win), lambda g: (g, 0, 0)),
            pl.BlockSpec(memory_space=pltpu.VMEM),
        ],
        out_specs=pl.BlockSpec((rounds, step_bins, 2, chan, chan), lambda g: (0, g, 0, 0, 0)),
        out_shape=jax.ShapeDtypeStruct((rounds, bins, 2, chan, chan), jnp.float32),
        cost_estimate=pl.CostEstimate(
            flops=2 * rounds * bins * two_chan * two_win * chan,
            bytes_accessed=lhs.size * 2 + arrived.size * 2 + rounds * bins * 2 * chan * chan * 4,
            transcendentals=0,
        ),
    )(lhs, pltpu.with_memory_space_constraint(arrived, pltpu.VMEM))


def pick_kernel(plan_ref, held_ref, out_hbm, sems):
    dests, rounds = out_hbm.shape[0], out_hbm.shape[1]
    copies = []
    for d in range(dests):
        for r in range(rounds):
            copy = pltpu.make_async_copy(held_ref.at[plan_ref[r, d]], out_hbm.at[d, r], sems.at[r, d])
            copy.start()
            copies.append(copy)
    for copy in copies:
        copy.wait()


def pick_partners(plan, held):
    rounds, dests = plan.shape
    _, rows, width = held.shape
    return pl.pallas_call(
        pick_kernel,
        in_specs=[pl.BlockSpec(memory_space=pltpu.SMEM), pl.BlockSpec(memory_space=pltpu.VMEM)],
        out_specs=pl.BlockSpec(memory_space=pl.ANY),
        out_shape=jax.ShapeDtypeStruct((dests, rounds, rows, width), held.dtype),
        scratch_shapes=[pltpu.SemaphoreType.DMA((rounds, dests))],
        cost_estimate=pl.CostEstimate(
            flops=0, bytes_accessed=held.size * 2 + dests * rounds * rows * width * 4, transcendentals=0
        ),
    )(plan, pltpu.with_memory_space_constraint(held, pltpu.VMEM))


def on_device(spectra, plan, assignment):
    bin_count, win_local, _, chan_width = spectra.shape
    seg_count = lax.axis_size("seg")
    group_count = lax.axis_size("chan")
    seg_index = lax.axis_index("seg")
    win_count = win_local * seg_count
    my_bins = bin_count // seg_count
    scale = 1.0 / math.sqrt(win_count)
    local_slots = assignment - lax.axis_index("chan") * chan_width
    onehot = (local_slots[None, :] == jnp.arange(chan_width, dtype=local_slots.dtype)[:, None])
    ordered = jnp.einsum(
        "fwkm,mc->fwkc", spectra, onehot.astype(spectra.dtype), preferred_element_type=jnp.float32
    ).astype(spectra.dtype)
    per_bin = group_count // my_bins
    win_piece = win_local // per_bin
    rows = ordered.reshape(seg_count, my_bins, per_bin, win_piece, 2 * chan_width)
    send = rows.transpose(1, 2, 0, 3, 4).reshape(group_count * seg_count, win_piece, 2 * chan_width)
    held = lax.all_to_all(send, ("chan", "seg"), split_axis=0, concat_axis=0, tiled=True)
    held = held.reshape(group_count, seg_count * win_piece, 2 * chan_width)
    outgoing = pick_partners(plan, held)
    arrived = lax.all_to_all(outgoing, "chan", split_axis=0, concat_axis=0, tiled=True)
    ranges = ordered.reshape(seg_count, my_bins, win_local, 2 * chan_width)
    by_shift = [lax.dynamic_index_in_dim(ranges, seg_index, 0, keepdims=False)]
    for shift in range(1, seg_count):
        part = lax.dynamic_index_in_dim(ranges, (seg_index + shift) % seg_count, 0, keepdims=False)
        pairs = [(i, (i + shift) % seg_count) for i in range(seg_count)]
        by_shift.append(lax.ppermute(part, "seg", pairs))
    by_shift = jnp.stack(by_shift)
    order = (seg_index - jnp.arange(seg_count)) % seg_count
    own = jnp.take(by_shift, order, axis=0)
    own = own.reshape(seg_count, my_bins, per_bin, win_piece, 2, chan_width)
    own = own.transpose(1, 5, 4, 2, 0, 3).reshape(my_bins, chan_width, 2, win_count)
    imag_rows = jnp.stack([own[:, :, 1], -own[:, :, 0]], axis=2)
    lhs = jnp.stack([own, imag_rows], axis=1).reshape(my_bins, 2 * chan_width, 2 * win_count)
    return cross_spectra(lhs, arrived, scale)


def solution(mesh):
    in_specs = (P(None, "seg", None, "chan"), P(), P("chan"))
    out_specs = P(None, "seg", None, "chan", None)
    return jax.shard_map(
        on_device, mesh=mesh, in_specs=in_specs, out_specs=out_specs, check_vma=False
    )
```

```python
import functools
import math

import jax
import jax.numpy as jnp
from jax import lax
from jax.experimental import pallas as pl
from jax.experimental.pallas import tpu as pltpu
from jax.sharding import PartitionSpec as P


def cross_kernel(scale, lhs_ref, rhs_ref, out_ref):
    step_bins = lhs_ref.shape[0]
    pieces, rounds, rows, two_chan = rhs_ref.shape
    per_bin = pieces // (step_bins * pl.num_programs(0))
    chan = two_chan // 2
    first = pl.program_id(0) * step_bins
    for b in range(step_bins):
        lhs = lhs_ref[b]
        for r0 in range(0, rounds, 2):
            columns = []
            for r in (r0, r0 + 1):
                block = rhs_ref[pl.ds((first + b) * per_bin, per_bin), r]
                block = block.reshape(per_bin * rows, two_chan)
                columns.append(jnp.concatenate([block[:, :chan], block[:, chan:]], axis=0))
            acc = jnp.dot(lhs, jnp.concatenate(columns, axis=1), preferred_element_type=jnp.float32)
            acc = acc * scale
            out_ref[r0, b] = acc[:, :chan].reshape(2, chan, chan)
            out_ref[r0 + 1, b] = acc[:, chan:].reshape(2, chan, chan)


def cross_spectra(lhs, arrived, scale):
    bins, two_chan, two_win = lhs.shape
    chan = two_chan // 2
    pieces, rounds, rows, _ = arrived.shape
    per_bin = pieces // bins
    step_bins = 4
    return pl.pallas_call(
        functools.partial(cross_kernel, scale),
        grid=(bins // step_bins,),
        in_specs=[
            pl.BlockSpec((step_bins, two_chan, two_win), lambda g: (g, 0, 0)),
            pl.BlockSpec(memory_space=pltpu.VMEM),
        ],
        out_specs=pl.BlockSpec((rounds, step_bins, 2, chan, chan), lambda g: (0, g, 0, 0, 0)),
        out_shape=jax.ShapeDtypeStruct((rounds, bins, 2, chan, chan), jnp.float32),
        cost_estimate=pl.CostEstimate(
            flops=2 * rounds * bins * two_chan * two_win * chan,
            bytes_accessed=lhs.size * 2 + arrived.size * 2 + rounds * bins * 2 * chan * chan * 4,
            transcendentals=0,
        ),
    )(lhs, pltpu.with_memory_space_constraint(arrived, pltpu.VMEM))


def pick_kernel(plan_ref, held_ref, out_ref):
    dests, rounds = out_ref.shape[0], out_ref.shape[1]
    for d in range(dests):
        for r in range(rounds):
            out_ref[d, r] = held_ref[plan_ref[r, d]]


def pick_partners(plan, held):
    rounds, dests = plan.shape
    _, rows, width = held.shape
    return pl.pallas_call(
        pick_kernel,
        in_specs=[pl.BlockSpec(memory_space=pltpu.SMEM), pl.BlockSpec(memory_space=pltpu.VMEM)],
        out_specs=pl.BlockSpec(memory_space=pltpu.VMEM),
        out_shape=jax.ShapeDtypeStruct((dests, rounds, rows, width), held.dtype),
        cost_estimate=pl.CostEstimate(
            flops=0, bytes_accessed=held.size * 2 + dests * rounds * rows * width * 4, transcendentals=0
        ),
    )(plan, pltpu.with_memory_space_constraint(held, pltpu.VMEM))


def on_device(spectra, plan, assignment):
    bin_count, win_local, _, chan_width = spectra.shape
    seg_count = lax.axis_size("seg")
    group_count = lax.axis_size("chan")
    seg_index = lax.axis_index("seg")
    win_count = win_local * seg_count
    my_bins = bin_count // seg_count
    scale = 1.0 / math.sqrt(win_count)
    local_slots = assignment - lax.axis_index("chan") * chan_width
    onehot = (local_slots[None, :] == jnp.arange(chan_width, dtype=local_slots.dtype)[:, None])
    ordered = jnp.einsum(
        "fwkm,mc->fwkc", spectra, onehot.astype(spectra.dtype), preferred_element_type=jnp.float32
    ).astype(spectra.dtype)
    per_bin = group_count // my_bins
    win_piece = win_local // per_bin
    rows = ordered.reshape(seg_count, my_bins, per_bin, win_piece, 2 * chan_width)
    send = rows.transpose(1, 2, 0, 3, 4).reshape(group_count * seg_count, win_piece, 2 * chan_width)
    held = lax.all_to_all(send, ("chan", "seg"), split_axis=0, concat_axis=0, tiled=True)
    held = held.reshape(group_count, seg_count * win_piece, 2 * chan_width)
    outgoing = pick_partners(plan, held)
    arrived = lax.all_to_all(outgoing, "chan", split_axis=0, concat_axis=0, tiled=True)
    ranges = ordered.reshape(seg_count, my_bins, win_local, 2 * chan_width)
    by_shift = [lax.dynamic_index_in_dim(ranges, seg_index, 0, keepdims=False)]
    for shift in range(1, seg_count):
        part = lax.dynamic_index_in_dim(ranges, (seg_index + shift) % seg_count, 0, keepdims=False)
        pairs = [(i, (i + shift) % seg_count) for i in range(seg_count)]
        by_shift.append(lax.ppermute(part, "seg", pairs))
    by_shift = jnp.stack(by_shift)
    order = (seg_index - jnp.arange(seg_count)) % seg_count
    own = jnp.take(by_shift, order, axis=0)
    own = own.reshape(seg_count, my_bins, per_bin, win_piece, 2, chan_width)
    own = own.transpose(1, 5, 4, 2, 0, 3).reshape(my_bins, chan_width, 2, win_count)
    imag_rows = jnp.stack([own[:, :, 1], -own[:, :, 0]], axis=2)
    lhs = jnp.stack([own, imag_rows], axis=1).reshape(my_bins, 2 * chan_width, 2 * win_count)
    return cross_spectra(lhs, arrived, scale)


def solution(mesh):
    in_specs = (P(None, "seg", None, "chan"), P(), P("chan"))
    out_specs = P(None, "seg", None, "chan", None)
    return jax.shard_map(
        on_device, mesh=mesh, in_specs=in_specs, out_specs=out_specs, check_vma=False
    )
```

```python
import functools
import math

import jax
import jax.numpy as jnp
from jax import lax
from jax.experimental import pallas as pl
from jax.experimental.pallas import tpu as pltpu
from jax.sharding import PartitionSpec as P


def cross_kernel(scale, lhs_ref, rhs_ref, out_ref):
    step_bins = lhs_ref.shape[0]
    pieces, rounds, rows, two_chan = rhs_ref.shape
    per_bin = pieces // (step_bins * pl.num_programs(0))
    chan = two_chan // 2
    first = pl.program_id(0) * step_bins
    for b in range(step_bins):
        lhs = lhs_ref[b]
        for r0 in range(0, rounds, 2):
            columns = []
            for r in (r0, r0 + 1):
                block = rhs_ref[pl.ds((first + b) * per_bin, per_bin), r]
                block = block.reshape(per_bin * rows, two_chan)
                columns.append(jnp.concatenate([block[:, :chan], block[:, chan:]], axis=0))
            acc = jnp.dot(lhs, jnp.concatenate(columns, axis=1), preferred_element_type=jnp.float32)
            acc = acc * scale
            out_ref[r0, b] = acc[:, :chan].reshape(2, chan, chan)
            out_ref[r0 + 1, b] = acc[:, chan:].reshape(2, chan, chan)


def cross_spectra(lhs, arrived, scale):
    bins, two_chan, two_win = lhs.shape
    chan = two_chan // 2
    pieces, rounds, rows, _ = arrived.shape
    per_bin = pieces // bins
    step_bins = 4
    return pl.pallas_call(
        functools.partial(cross_kernel, scale),
        grid=(bins // step_bins,),
        in_specs=[
            pl.BlockSpec((step_bins, two_chan, two_win), lambda g: (g, 0, 0)),
            pl.BlockSpec(memory_space=pltpu.VMEM),
        ],
        out_specs=pl.BlockSpec((rounds, step_bins, 2, chan, chan), lambda g: (0, g, 0, 0, 0)),
        out_shape=jax.ShapeDtypeStruct((rounds, bins, 2, chan, chan), jnp.float32),
        cost_estimate=pl.CostEstimate(
            flops=2 * rounds * bins * two_chan * two_win * chan,
            bytes_accessed=lhs.size * 2 + arrived.size * 2 + rounds * bins * 2 * chan * chan * 4,
            transcendentals=0,
        ),
    )(lhs, pltpu.with_memory_space_constraint(arrived, pltpu.VMEM))


def pick_kernel(plan_ref, held_ref, out_hbm, staged, sems):
    groups, per_group, rounds = staged.shape[0], staged.shape[1], staged.shape[2]
    copies = []
    for g in range(groups):
        for d in range(per_group):
            for r in range(rounds):
                staged[g, d, r] = held_ref[plan_ref[r, g * per_group + d]]
        copy = pltpu.make_async_copy(staged.at[g], out_hbm.at[pl.ds(g * per_group, per_group)], sems.at[g])
        copy.start()
        copies.append(copy)
    for copy in copies:
        copy.wait()


def pick_partners(plan, held):
    rounds, dests = plan.shape
    _, rows, width = held.shape
    groups = 4
    return pl.pallas_call(
        pick_kernel,
        in_specs=[pl.BlockSpec(memory_space=pltpu.SMEM), pl.BlockSpec(memory_space=pltpu.VMEM)],
        out_specs=pl.BlockSpec(memory_space=pl.ANY),
        out_shape=jax.ShapeDtypeStruct((dests, rounds, rows, width), held.dtype),
        scratch_shapes=[
            pltpu.VMEM((groups, dests // groups, rounds, rows, width), held.dtype),
            pltpu.SemaphoreType.DMA((groups,)),
        ],
        cost_estimate=pl.CostEstimate(
            flops=0, bytes_accessed=held.size * 2 + dests * rounds * rows * width * 4, transcendentals=0
        ),
    )(plan, pltpu.with_memory_space_constraint(held, pltpu.VMEM))


def on_device(spectra, plan, assignment):
    bin_count, win_local, _, chan_width = spectra.shape
    seg_count = lax.axis_size("seg")
    group_count = lax.axis_size("chan")
    seg_index = lax.axis_index("seg")
    win_count = win_local * seg_count
    my_bins = bin_count // seg_count
    scale = 1.0 / math.sqrt(win_count)
    local_slots = assignment - lax.axis_index("chan") * chan_width
    onehot = (local_slots[None, :] == jnp.arange(chan_width, dtype=local_slots.dtype)[:, None])
    ordered = jnp.einsum(
        "fwkm,mc->fwkc", spectra, onehot.astype(spectra.dtype), preferred_element_type=jnp.float32
    ).astype(spectra.dtype)
    per_bin = group_count // my_bins
    win_piece = win_local // per_bin
    rows = ordered.reshape(seg_count, my_bins, per_bin, win_piece, 2 * chan_width)
    send = rows.transpose(1, 2, 0, 3, 4).reshape(group_count * seg_count, win_piece, 2 * chan_width)
    held = lax.all_to_all(send, ("chan", "seg"), split_axis=0, concat_axis=0, tiled=True)
    held = held.reshape(group_count, seg_count * win_piece, 2 * chan_width)
    outgoing = pick_partners(plan, held)
    arrived = lax.all_to_all(outgoing, "chan", split_axis=0, concat_axis=0, tiled=True)
    ranges = ordered.reshape(seg_count, my_bins, win_local, 2 * chan_width)
    by_shift = [lax.dynamic_index_in_dim(ranges, seg_index, 0, keepdims=False)]
    for shift in range(1, seg_count):
        part = lax.dynamic_index_in_dim(ranges, (seg_index + shift) % seg_count, 0, keepdims=False)
        pairs = [(i, (i + shift) % seg_count) for i in range(seg_count)]
        by_shift.append(lax.ppermute(part, "seg", pairs))
    by_shift = jnp.stack(by_shift)
    order = (seg_index - jnp.arange(seg_count)) % seg_count
    own = jnp.take(by_shift, order, axis=0)
    own = own.reshape(seg_count, my_bins, per_bin, win_piece, 2, chan_width)
    own = own.transpose(1, 5, 4, 2, 0, 3).reshape(my_bins, chan_width, 2, win_count)
    imag_rows = jnp.stack([own[:, :, 1], -own[:, :, 0]], axis=2)
    lhs = jnp.stack([own, imag_rows], axis=1).reshape(my_bins, 2 * chan_width, 2 * win_count)
    return cross_spectra(lhs, arrived, scale)


def solution(mesh):
    in_specs = (P(None, "seg", None, "chan"), P(), P("chan"))
    out_specs = P(None, "seg", None, "chan", None)
    return jax.shard_map(
        on_device, mesh=mesh, in_specs=in_specs, out_specs=out_specs, check_vma=False
    )
```

```python
import functools
import math

import jax
import jax.numpy as jnp
from jax import lax
from jax.experimental import pallas as pl
from jax.experimental.pallas import tpu as pltpu
from jax.sharding import PartitionSpec as P


def cross_kernel(scale, lhs_ref, rhs_ref, out_ref):
    step_bins = lhs_ref.shape[0]
    pieces, rounds, rows, two_chan = rhs_ref.shape
    per_bin = pieces // (step_bins * pl.num_programs(0))
    chan = two_chan // 2
    first = pl.program_id(0) * step_bins
    for b in range(step_bins):
        lhs = lhs_ref[b]
        for r0 in range(0, rounds, 2):
            columns = []
            for r in (r0, r0 + 1):
                block = rhs_ref[pl.ds((first + b) * per_bin, per_bin), r]
                block = block.reshape(per_bin * rows, two_chan)
                columns.append(jnp.concatenate([block[:, :chan], block[:, chan:]], axis=0))
            acc = jnp.dot(lhs, jnp.concatenate(columns, axis=1), preferred_element_type=jnp.float32)
            acc = acc * scale
            out_ref[r0, b] = acc[:, :chan].reshape(2, chan, chan)
            out_ref[r0 + 1, b] = acc[:, chan:].reshape(2, chan, chan)


def cross_spectra(lhs, arrived, scale):
    bins, two_chan, two_win = lhs.shape
    chan = two_chan // 2
    pieces, rounds, rows, _ = arrived.shape
    per_bin = pieces // bins
    step_bins = 4
    return pl.pallas_call(
        functools.partial(cross_kernel, scale),
        grid=(bins // step_bins,),
        in_specs=[
            pl.BlockSpec((step_bins, two_chan, two_win), lambda g: (g, 0, 0)),
            pl.BlockSpec(memory_space=pltpu.VMEM),
        ],
        out_specs=pl.BlockSpec((rounds, step_bins, 2, chan, chan), lambda g: (0, g, 0, 0, 0)),
        out_shape=jax.ShapeDtypeStruct((rounds, bins, 2, chan, chan), jnp.float32),
        cost_estimate=pl.CostEstimate(
            flops=2 * rounds * bins * two_chan * two_win * chan,
            bytes_accessed=lhs.size * 2 + arrived.size * 2 + rounds * bins * 2 * chan * chan * 4,
            transcendentals=0,
        ),
    )(lhs, pltpu.with_memory_space_constraint(arrived, pltpu.VMEM))


def pick_kernel(plan_ref, held_ref, out_hbm, staged, sems):
    groups, per_group, rounds = staged.shape[0], staged.shape[1], staged.shape[2]
    copies = []
    for g in range(groups):
        for d in range(per_group):
            for r in range(rounds):
                staged[g, d, r] = held_ref[plan_ref[r, g * per_group + d]]
        copy = pltpu.make_async_copy(staged.at[g], out_hbm.at[pl.ds(g * per_group, per_group)], sems.at[g])
        copy.start()
        copies.append(copy)
    for copy in copies:
        copy.wait()


def pick_partners(plan, held):
    rounds, dests = plan.shape
    _, rows, width = held.shape
    groups = 8
    return pl.pallas_call(
        pick_kernel,
        in_specs=[pl.BlockSpec(memory_space=pltpu.SMEM), pl.BlockSpec(memory_space=pltpu.VMEM)],
        out_specs=pl.BlockSpec(memory_space=pl.ANY),
        out_shape=jax.ShapeDtypeStruct((dests, rounds, rows, width), held.dtype),
        scratch_shapes=[
            pltpu.VMEM((groups, dests // groups, rounds, rows, width), held.dtype),
            pltpu.SemaphoreType.DMA((groups,)),
        ],
        cost_estimate=pl.CostEstimate(
            flops=0, bytes_accessed=held.size * 2 + dests * rounds * rows * width * 4, transcendentals=0
        ),
    )(plan, pltpu.with_memory_space_constraint(held, pltpu.VMEM))


def on_device(spectra, plan, assignment):
    bin_count, win_local, _, chan_width = spectra.shape
    seg_count = lax.axis_size("seg")
    group_count = lax.axis_size("chan")
    seg_index = lax.axis_index("seg")
    win_count = win_local * seg_count
    my_bins = bin_count // seg_count
    scale = 1.0 / math.sqrt(win_count)
    local_slots = assignment - lax.axis_index("chan") * chan_width
    onehot = (local_slots[None, :] == jnp.arange(chan_width, dtype=local_slots.dtype)[:, None])
    ordered = jnp.einsum(
        "fwkm,mc->fwkc", spectra, onehot.astype(spectra.dtype), preferred_element_type=jnp.float32
    ).astype(spectra.dtype)
    per_bin = group_count // my_bins
    win_piece = win_local // per_bin
    rows = ordered.reshape(seg_count, my_bins, per_bin, win_piece, 2 * chan_width)
    send = rows.transpose(1, 2, 0, 3, 4).reshape(group_count * seg_count, win_piece, 2 * chan_width)
    held = lax.all_to_all(send, ("chan", "seg"), split_axis=0, concat_axis=0, tiled=True)
    held = held.reshape(group_count, seg_count * win_piece, 2 * chan_width)
    outgoing = pick_partners(plan, held)
    arrived = lax.all_to_all(outgoing, "chan", split_axis=0, concat_axis=0, tiled=True)
    ranges = ordered.reshape(seg_count, my_bins, win_local, 2 * chan_width)
    by_shift = [lax.dynamic_index_in_dim(ranges, seg_index, 0, keepdims=False)]
    for shift in range(1, seg_count):
        part = lax.dynamic_index_in_dim(ranges, (seg_index + shift) % seg_count, 0, keepdims=False)
        pairs = [(i, (i + shift) % seg_count) for i in range(seg_count)]
        by_shift.append(lax.ppermute(part, "seg", pairs))
    by_shift = jnp.stack(by_shift)
    order = (seg_index - jnp.arange(seg_count)) % seg_count
    own = jnp.take(by_shift, order, axis=0)
    own = own.reshape(seg_count, my_bins, per_bin, win_piece, 2, chan_width)
    own = own.transpose(1, 5, 4, 2, 0, 3).reshape(my_bins, chan_width, 2, win_count)
    imag_rows = jnp.stack([own[:, :, 1], -own[:, :, 0]], axis=2)
    lhs = jnp.stack([own, imag_rows], axis=1).reshape(my_bins, 2 * chan_width, 2 * win_count)
    return cross_spectra(lhs, arrived, scale)


def solution(mesh):
    in_specs = (P(None, "seg", None, "chan"), P(), P("chan"))
    out_specs = P(None, "seg", None, "chan", None)
    return jax.shard_map(
        on_device, mesh=mesh, in_specs=in_specs, out_specs=out_specs, check_vma=False
    )
```

```python
import functools
import math

import jax
import jax.numpy as jnp
from jax import lax
from jax.experimental import pallas as pl
from jax.experimental.pallas import tpu as pltpu
from jax.sharding import PartitionSpec as P


def cross_kernel(scale, lhs_ref, rhs_ref, out_ref):
    step_bins = lhs_ref.shape[0]
    pieces, rounds, rows, two_chan = rhs_ref.shape
    per_bin = pieces // (step_bins * pl.num_programs(0))
    chan = two_chan // 2
    first = pl.program_id(0) * step_bins
    for b in range(step_bins):
        real_rows = lhs_ref[b]
        half = real_rows.shape[1] // 2
        imag_rows = jnp.concatenate([real_rows[:, half:], -real_rows[:, :half]], axis=1)
        lhs = jnp.concatenate([real_rows, imag_rows], axis=0)
        for r0 in range(0, rounds, 2):
            columns = []
            for r in (r0, r0 + 1):
                block = rhs_ref[pl.ds((first + b) * per_bin, per_bin), r]
                block = block.reshape(per_bin * rows, two_chan)
                columns.append(jnp.concatenate([block[:, :chan], block[:, chan:]], axis=0))
            acc = jnp.dot(lhs, jnp.concatenate(columns, axis=1), preferred_element_type=jnp.float32)
            acc = acc * scale
            out_ref[r0, b] = acc[:, :chan].reshape(2, chan, chan)
            out_ref[r0 + 1, b] = acc[:, chan:].reshape(2, chan, chan)


def cross_spectra(lhs, arrived, scale):
    bins, chan, two_win = lhs.shape
    two_chan = 2 * chan
    pieces, rounds, rows, _ = arrived.shape
    per_bin = pieces // bins
    step_bins = 4
    return pl.pallas_call(
        functools.partial(cross_kernel, scale),
        grid=(bins // step_bins,),
        in_specs=[
            pl.BlockSpec((step_bins, chan, two_win), lambda g: (g, 0, 0)),
            pl.BlockSpec(memory_space=pltpu.VMEM),
        ],
        out_specs=pl.BlockSpec((rounds, step_bins, 2, chan, chan), lambda g: (0, g, 0, 0, 0)),
        out_shape=jax.ShapeDtypeStruct((rounds, bins, 2, chan, chan), jnp.float32),
        cost_estimate=pl.CostEstimate(
            flops=2 * rounds * bins * two_chan * two_win * chan,
            bytes_accessed=lhs.size * 2 + arrived.size * 2 + rounds * bins * 2 * chan * chan * 4,
            transcendentals=0,
        ),
    )(lhs, pltpu.with_memory_space_constraint(arrived, pltpu.VMEM))


def pick_kernel(plan_ref, held_ref, out_hbm, staged, sems):
    groups, per_group, rounds = staged.shape[0], staged.shape[1], staged.shape[2]
    copies = []
    for g in range(groups):
        for d in range(per_group):
            for r in range(rounds):
                staged[g, d, r] = held_ref[plan_ref[r, g * per_group + d]]
        copy = pltpu.make_async_copy(staged.at[g], out_hbm.at[pl.ds(g * per_group, per_group)], sems.at[g])
        copy.start()
        copies.append(copy)
    for copy in copies:
        copy.wait()


def pick_partners(plan, held):
    rounds, dests = plan.shape
    _, rows, width = held.shape
    groups = 4
    return pl.pallas_call(
        pick_kernel,
        in_specs=[pl.BlockSpec(memory_space=pltpu.SMEM), pl.BlockSpec(memory_space=pltpu.VMEM)],
        out_specs=pl.BlockSpec(memory_space=pl.ANY),
        out_shape=jax.ShapeDtypeStruct((dests, rounds, rows, width), held.dtype),
        scratch_shapes=[
            pltpu.VMEM((groups, dests // groups, rounds, rows, width), held.dtype),
            pltpu.SemaphoreType.DMA((groups,)),
        ],
        cost_estimate=pl.CostEstimate(
            flops=0, bytes_accessed=held.size * 2 + dests * rounds * rows * width * 4, transcendentals=0
        ),
    )(plan, pltpu.with_memory_space_constraint(held, pltpu.VMEM))


def on_device(spectra, plan, assignment):
    bin_count, win_local, _, chan_width = spectra.shape
    seg_count = lax.axis_size("seg")
    group_count = lax.axis_size("chan")
    seg_index = lax.axis_index("seg")
    win_count = win_local * seg_count
    my_bins = bin_count // seg_count
    scale = 1.0 / math.sqrt(win_count)
    local_slots = assignment - lax.axis_index("chan") * chan_width
    onehot = (local_slots[None, :] == jnp.arange(chan_width, dtype=local_slots.dtype)[:, None])
    ordered = jnp.einsum(
        "fwkm,mc->fwkc", spectra, onehot.astype(spectra.dtype), preferred_element_type=jnp.float32
    ).astype(spectra.dtype)
    per_bin = group_count // my_bins
    win_piece = win_local // per_bin
    rows = ordered.reshape(seg_count, my_bins, per_bin, win_piece, 2 * chan_width)
    send = rows.transpose(1, 2, 0, 3, 4).reshape(group_count * seg_count, win_piece, 2 * chan_width)
    held = lax.all_to_all(send, ("chan", "seg"), split_axis=0, concat_axis=0, tiled=True)
    held = held.reshape(group_count, seg_count * win_piece, 2 * chan_width)
    outgoing = pick_partners(plan, held)
    arrived = lax.all_to_all(outgoing, "chan", split_axis=0, concat_axis=0, tiled=True)
    ranges = ordered.reshape(seg_count, my_bins, win_local, 2 * chan_width)
    by_shift = [lax.dynamic_index_in_dim(ranges, seg_index, 0, keepdims=False)]
    for shift in range(1, seg_count):
        part = lax.dynamic_index_in_dim(ranges, (seg_index + shift) % seg_count, 0, keepdims=False)
        pairs = [(i, (i + shift) % seg_count) for i in range(seg_count)]
        by_shift.append(lax.ppermute(part, "seg", pairs))
    by_shift = jnp.stack(by_shift)
    order = (seg_index - jnp.arange(seg_count)) % seg_count
    own = jnp.take(by_shift, order, axis=0)
    own = own.reshape(seg_count, my_bins, per_bin, win_piece, 2, chan_width)
    own = own.transpose(1, 5, 4, 2, 0, 3).reshape(my_bins, chan_width, 2, win_count)
    return cross_spectra(own.reshape(my_bins, chan_width, 2 * win_count), arrived, scale)


def solution(mesh):
    in_specs = (P(None, "seg", None, "chan"), P(), P("chan"))
    out_specs = P(None, "seg", None, "chan", None)
    return jax.shard_map(
        on_device, mesh=mesh, in_specs=in_specs, out_specs=out_specs, check_vma=False
    )
```

```python
import functools
import math

import jax
import jax.numpy as jnp
from jax import lax
from jax.experimental import pallas as pl
from jax.experimental.pallas import tpu as pltpu
from jax.sharding import PartitionSpec as P


def cross_kernel(scale, lhs_ref, rhs_ref, out_ref):
    step_bins = lhs_ref.shape[0]
    pieces, rounds, rows, two_chan = rhs_ref.shape
    per_bin = pieces // (step_bins * pl.num_programs(0))
    chan = two_chan // 2
    first = pl.program_id(0) * step_bins
    for b in range(step_bins):
        real_rows = lhs_ref[b]
        half = real_rows.shape[1] // 2
        imag_rows = jnp.concatenate([real_rows[:, half:], -real_rows[:, :half]], axis=1)
        lhs = jnp.concatenate([real_rows, imag_rows], axis=0)
        for r0 in range(0, rounds, 2):
            columns = []
            for r in (r0, r0 + 1):
                block = rhs_ref[pl.ds((first + b) * per_bin, per_bin), r]
                block = block.reshape(per_bin * rows, two_chan)
                columns.append(jnp.concatenate([block[:, :chan], block[:, chan:]], axis=0))
            acc = jnp.dot(lhs, jnp.concatenate(columns, axis=1), preferred_element_type=jnp.float32)
            acc = acc * scale
            out_ref[r0, b] = acc[:, :chan].reshape(2, chan, chan)
            out_ref[r0 + 1, b] = acc[:, chan:].reshape(2, chan, chan)


def cross_spectra(lhs, arrived, scale):
    bins, chan, two_win = lhs.shape
    two_chan = 2 * chan
    pieces, rounds, rows, _ = arrived.shape
    per_bin = pieces // bins
    step_bins = 2
    return pl.pallas_call(
        functools.partial(cross_kernel, scale),
        grid=(bins // step_bins,),
        in_specs=[
            pl.BlockSpec((step_bins, chan, two_win), lambda g: (g, 0, 0)),
            pl.BlockSpec(memory_space=pltpu.VMEM),
        ],
        out_specs=pl.BlockSpec((rounds, step_bins, 2, chan, chan), lambda g: (0, g, 0, 0, 0)),
        out_shape=jax.ShapeDtypeStruct((rounds, bins, 2, chan, chan), jnp.float32),
        cost_estimate=pl.CostEstimate(
            flops=2 * rounds * bins * two_chan * two_win * chan,
            bytes_accessed=lhs.size * 2 + arrived.size * 2 + rounds * bins * 2 * chan * chan * 4,
            transcendentals=0,
        ),
    )(lhs, pltpu.with_memory_space_constraint(arrived, pltpu.VMEM))


def pick_kernel(plan_ref, held_ref, out_hbm, staged, sems):
    groups, per_group, rounds = staged.shape[0], staged.shape[1], staged.shape[2]
    copies = []
    for g in range(groups):
        for d in range(per_group):
            for r in range(rounds):
                staged[g, d, r] = held_ref[plan_ref[r, g * per_group + d]]
        copy = pltpu.make_async_copy(staged.at[g], out_hbm.at[pl.ds(g * per_group, per_group)], sems.at[g])
        copy.start()
        copies.append(copy)
    for copy in copies:
        copy.wait()


def pick_partners(plan, held):
    rounds, dests = plan.shape
    _, rows, width = held.shape
    groups = 4
    return pl.pallas_call(
        pick_kernel,
        in_specs=[pl.BlockSpec(memory_space=pltpu.SMEM), pl.BlockSpec(memory_space=pltpu.VMEM)],
        out_specs=pl.BlockSpec(memory_space=pl.ANY),
        out_shape=jax.ShapeDtypeStruct((dests, rounds, rows, width), held.dtype),
        scratch_shapes=[
            pltpu.VMEM((groups, dests // groups, rounds, rows, width), held.dtype),
            pltpu.SemaphoreType.DMA((groups,)),
        ],
        cost_estimate=pl.CostEstimate(
            flops=0, bytes_accessed=held.size * 2 + dests * rounds * rows * width * 4, transcendentals=0
        ),
    )(plan, pltpu.with_memory_space_constraint(held, pltpu.VMEM))


def on_device(spectra, plan, assignment):
    bin_count, win_local, _, chan_width = spectra.shape
    seg_count = lax.axis_size("seg")
    group_count = lax.axis_size("chan")
    seg_index = lax.axis_index("seg")
    win_count = win_local * seg_count
    my_bins = bin_count // seg_count
    scale = 1.0 / math.sqrt(win_count)
    local_slots = assignment - lax.axis_index("chan") * chan_width
    onehot = (local_slots[None, :] == jnp.arange(chan_width, dtype=local_slots.dtype)[:, None])
    ordered = jnp.einsum(
        "fwkm,mc->fwkc", spectra, onehot.astype(spectra.dtype), preferred_element_type=jnp.float32
    ).astype(spectra.dtype)
    per_bin = group_count // my_bins
    win_piece = win_local // per_bin
    rows = ordered.reshape(seg_count, my_bins, per_bin, win_piece, 2 * chan_width)
    send = rows.transpose(1, 2, 0, 3, 4).reshape(group_count * seg_count, win_piece, 2 * chan_width)
    held = lax.all_to_all(send, ("chan", "seg"), split_axis=0, concat_axis=0, tiled=True)
    held = held.reshape(group_count, seg_count * win_piece, 2 * chan_width)
    outgoing = pick_partners(plan, held)
    arrived = lax.all_to_all(outgoing, "chan", split_axis=0, concat_axis=0, tiled=True)
    ranges = ordered.reshape(seg_count, my_bins, win_local, 2 * chan_width)
    by_shift = [lax.dynamic_index_in_dim(ranges, seg_index, 0, keepdims=False)]
    for shift in range(1, seg_count):
        part = lax.dynamic_index_in_dim(ranges, (seg_index + shift) % seg_count, 0, keepdims=False)
        pairs = [(i, (i + shift) % seg_count) for i in range(seg_count)]
        by_shift.append(lax.ppermute(part, "seg", pairs))
    by_shift = jnp.stack(by_shift)
    order = (seg_index - jnp.arange(seg_count)) % seg_count
    own = jnp.take(by_shift, order, axis=0)
    own = own.reshape(seg_count, my_bins, per_bin, win_piece, 2, chan_width)
    own = own.transpose(1, 5, 4, 2, 0, 3).reshape(my_bins, chan_width, 2, win_count)
    return cross_spectra(own.reshape(my_bins, chan_width, 2 * win_count), arrived, scale)


def solution(mesh):
    in_specs = (P(None, "seg", None, "chan"), P(), P("chan"))
    out_specs = P(None, "seg", None, "chan", None)
    return jax.shard_map(
        on_device, mesh=mesh, in_specs=in_specs, out_specs=out_specs, check_vma=False
    )
```
